256 devices in a mesh: dp: 128 (over x, y_lo, z, core), section: 2 (over y_hi).
Axes of the slice: x: 4, y: 4 (y_hi: 2, y_lo: 2; y = y_hi * 2 + y_lo), z: 8, core: 2. Of those that a mesh axis runs over, the one named last changes fastest.
Arguments:
- replay_rows: bfloat16 [65536, 4, 4, 128], P('dp'), may hold values from -6 to 6
- qvalues: bfloat16 [65536, 18], P('dp'), may hold values from -5 to 129
- target_logits: bfloat16 [65536, 18], P('dp'), may hold values from -8 to 258
- replay_owner: int32 [32768], P(('dp', 'section')), may hold values from 0 to 127, as said below
- replay_slot: int32 [32768], P(('dp', 'section')), may hold values from 0 to 511
- sample_actions: int32 [32768, 20], P(('dp', 'section')), may hold values from 0 to 17
- weights: bfloat16 [2, 147456], replicated, may hold values from -0.1875 to 0.1875
- head: bfloat16 [128, 18], replicated, may hold values from -0.5 to 0.5
- master: float32 [2, 147456], P('section', 'dp'), may hold values from -0.0012 to 0.0012
- moment_first: float32 [2, 147456], P('section', 'dp'), may hold values from -0.0021 to 0.0021
- moment_second: float32 [2, 147456], P('section', 'dp'), may hold values from 9.9e-14 to 1.01e-06
Outputs:
- adam_step: float32 [2, 147456], P('section', 'dp')
- new_weights: bfloat16 [2, 147456], replicated
The draws below stay inside these ranges and needn't reach their ends.
Inputs may be any that keep to these rules, and one draw needn't show every extreme that they name: `replay_owner`: among the 128 rows of one learner device no shard is named more than 2 times; in every draw one shard is named exactly 2 times by every learner device.
All inputs are finite; a program needn't handle non-finite values.
Results may differ from the reference program's by a relative error of at most 0.013.
Values may be sent and summed in bfloat16 or wider, within the bound.
No kernel may reach another device: no remote copies, remote signals or barrier semaphores. Data moves between devices by JAX's collectives and lax.ppermute only.
A program may use at most 192 MiB of HBM per device.

```python
import math
import jax
import jax.numpy as jnp
from jax import lax

CHANNELS = 128
GRID = 4
ACTIONS = 18
SAMPLES = 20
BATCH_DEV = 128
REPLAY_DEV = 512
CAP = 2
LEARN_ROWS = 32768
REPLAY = 65536
PARAMS = 147456
N_DP = 128
N_SECTION = 2


def draw_qvalues(key, part):
    noise = jnp.clip(jax.random.normal(jax.random.fold_in(key, 11), (REPLAY, ACTIONS), jnp.float32), -5.0, 5.0)
    values = noise
    return values.astype(jnp.bfloat16)


def draw_target_logits(key, part):
    noise = jnp.clip(jax.random.normal(jax.random.fold_in(key, 14), (REPLAY, ACTIONS), jnp.float32), -5.0, 5.0)
    values = 1.5 * noise
    return values.astype(jnp.bfloat16)


def draw_replay_owner(key, part):
    learner_group = N_DP * N_SECTION
    total = CAP * N_DP
    hot_owner = jax.random.randint(jax.random.fold_in(key, 1), (), 0, N_DP)
    keys = jax.random.split(jax.random.fold_in(key, 2), learner_group)
    candidate = jnp.arange(total, dtype=jnp.int32) % N_DP

    def one_learner(learner_key):
        key_order = jax.random.fold_in(learner_key, 3)
        key_shuffle = jax.random.fold_in(learner_key, 4)
        shuffled = jax.random.permutation(key_order, total).astype(jnp.int32)
        move_logit_matrix = jnp.where(candidate == hot_owner, -1 - jnp.arange(total, dtype=jnp.int32), shuffled)
        selected_moves = candidate[jnp.argsort(move_logit_matrix, stable=True)[:BATCH_DEV]]
        return selected_moves[jax.random.permutation(key_shuffle, BATCH_DEV)]
    return jax.vmap(one_learner)(keys).reshape(-1).astype(jnp.int32)


def draw_master(key, part):
    base = jax.random.fold_in(key, 31)
    values = 0.0003 * jnp.clip(jax.random.normal(jax.random.fold_in(base, 2), (2, PARAMS), jnp.float32), -4.0, 4.0)
    return values


def moment_pair(key):
    base = jax.random.fold_in(key, 21)
    exponent = jax.random.uniform(jax.random.fold_in(base, 1), (2, PARAMS), jnp.float32, -13.0, -6.0)
    second = jnp.exp(exponent * math.log(10.0))
    noise = jnp.clip(jax.random.normal(jax.random.fold_in(base, 2), (2, PARAMS), jnp.float32), -4.0, 4.0)
    first = 0.5 * jnp.sqrt(second) * noise
    return (first, second)


def draw_moment_first(key, part):
    return moment_pair(key)[0]


def draw_moment_second(key, part):
    return moment_pair(key)[1]


def set_ends(array, own_key, smallest, high):
    place = [jax.random.randint(jax.random.fold_in(own_key, axis), (), 0, length) for axis, length in enumerate(array.shape)]
    longest = array.shape.index(max(array.shape))
    neighbour = place[:longest] + [(place[longest] + 1) % array.shape[longest]] + place[longest + 1:]
    return array.at[tuple(place)].set(smallest).at[tuple(neighbour)].set(high)


def levels(key, shape, cuts, least, largest):
    def one(position, parts):
        draws = jax.random.uniform(jax.random.fold_in(jax.random.fold_in(key, 6), position), (parts,), jnp.float32, least / len(cuts), largest / len(cuts))
        return jnp.repeat(jnp.exp(draws), shape[position] // parts).reshape((-1,) + (1,) * (len(shape) - position - 1))

    loudness = one(*cuts[0])
    for cut in cuts[1:]:
        loudness = loudness * one(*cut)
    return loudness


def scatter_about(rng, extent, deviation, most, pieces=(), kind=jnp.bfloat16):
    result = jax.random.normal(rng, extent, jnp.float32) * deviation
    if len(pieces) > 0:
        result = levels(rng, extent, pieces, -0.22, 0.18) * result
    return jnp.clip(result, min=-most, max=most).astype(kind)


def setup_inputs(seed: int = 0) -> dict:
    key_list = jax.random.split(jax.random.key(seed), 12)
    replay_rows = scatter_about(key_list[0], (REPLAY, GRID, GRID, CHANNELS), 1.0, 6.0, ((0, 128),))
    qvalues = draw_qvalues(jax.random.fold_in(key_list[11], 71), 0)
    target_logits = draw_target_logits(jax.random.fold_in(key_list[11], 71), 0)
    replay_owner = draw_replay_owner(jax.random.fold_in(key_list[11], 71), 0)
    replay_slot = set_ends(jax.random.randint(key_list[4], (LEARN_ROWS,), 0, REPLAY_DEV), jax.random.fold_in(key_list[4], 1), 0, REPLAY_DEV - 1).astype(jnp.int32)
    sample_actions = set_ends(jax.random.randint(key_list[5], (LEARN_ROWS, SAMPLES), 0, ACTIONS), jax.random.fold_in(key_list[5], 1), 0, ACTIONS - 1).astype(jnp.int32)
    weights = scatter_about(key_list[6], (2, PARAMS), (9 * CHANNELS) ** -0.5, 0.1875)
    head = scatter_about(key_list[7], (CHANNELS, ACTIONS), CHANNELS ** -0.5, 0.5)
    master = draw_master(jax.random.fold_in(key_list[11], 71), 0)
    moment_first = draw_moment_first(jax.random.fold_in(key_list[11], 71), 0)
    moment_second = draw_moment_second(jax.random.fold_in(key_list[11], 71), 0)
    return dict(replay_rows=replay_rows, qvalues=qvalues, target_logits=target_logits, replay_owner=replay_owner, replay_slot=replay_slot, sample_actions=sample_actions, weights=weights, head=head, master=master, moment_first=moment_first, moment_second=moment_second)


constant_entropy_scale = 0.5
trust_weight = 0.5
beta_first = 0.9
beta_second = 0.999
epsilon = 1e-08
learn_rate = 0.0001

def tap_stack(field):
    grid_side = field.shape[1]
    padded_rows = jnp.pad(field, ((0, 0), (1, 1), (1, 1), (0, 0)))
    return jnp.concatenate([padded_rows[:, shift_row:shift_row + grid_side, shift_col:shift_col + grid_side, :] for shift_row in range(3) for shift_col in range(3)], axis=-1)

def layer_grads(features, move_return_estimates, reference_policy_entries, actions, row_scale, w_first, second_weight, head):
    row_count, grid_side, _, channels = features.shape
    positions = row_count * grid_side * grid_side
    taps_first = tap_stack(features).reshape(positions, 9 * channels)
    hidden = jax.nn.relu(jnp.dot(taps_first, w_first, preferred_element_type=jnp.float32)).astype(jnp.bfloat16)
    taps_second = tap_stack(hidden.reshape(features.shape)).reshape(positions, 9 * channels)
    summed = features.reshape(positions, channels).astype(jnp.float32) + jnp.dot(taps_second, second_weight, preferred_element_type=jnp.float32)
    block_out = jax.nn.relu(summed).astype(jnp.bfloat16)
    averaged_embedding = lax.optimization_barrier(jnp.mean(block_out.astype(jnp.float32).reshape(row_count, grid_side * grid_side, channels), axis=1)).astype(jnp.bfloat16)
    logits = reference_policy_entries.astype(jnp.float32) + jnp.dot(averaged_embedding, head, preferred_element_type=jnp.float32)
    policy = jax.nn.softmax(logits, axis=-1)
    prior = jax.nn.softmax(reference_policy_entries.astype(jnp.float32), axis=-1)
    selected_moves = (actions[:, :, None] == jnp.arange(head.shape[1])[None, None, :]).astype(jnp.float32)
    move_logit_matrix = jnp.einsum('vlu,vu->vl', selected_moves, move_return_estimates.astype(jnp.float32)) / constant_entropy_scale
    sample_weight = jax.nn.softmax(move_logit_matrix, axis=-1)
    logit_grad = ((1.0 + trust_weight) * policy - jnp.einsum('nk,nka->na', sample_weight, selected_moves) - trust_weight * prior) * row_scale[:, None]
    pooled_grad = jnp.dot(logit_grad, head.astype(jnp.float32).T, precision=lax.Precision.HIGHEST)
    spread = jnp.broadcast_to((pooled_grad / (grid_side * grid_side))[:, None, :], (row_count, grid_side * grid_side, channels)).reshape(positions, channels)
    out_grad = jnp.where(block_out > 0, spread, 0.0).astype(jnp.bfloat16)
    grad_second = lax.dot_general(taps_second, out_grad, (((0,), (0,)), ((), ())), preferred_element_type=jnp.float32)
    flipped = second_weight.reshape(9, channels, channels)[::-1].transpose(0, 2, 1).reshape(9 * channels, channels)
    taps_back = tap_stack(out_grad.reshape(features.shape)).reshape(positions, 9 * channels)
    hidden_grad = jnp.where(hidden > 0, jnp.dot(taps_back, flipped, preferred_element_type=jnp.float32), 0.0).astype(jnp.bfloat16)
    grad_first = lax.dot_general(taps_first, hidden_grad, (((0,), (0,)), ((), ())), preferred_element_type=jnp.float32)
    return (grad_first, grad_second)

def reference(replay_rows, qvalues, target_logits, replay_owner, replay_slot, sample_actions, weights, head, master, moment_first, moment_second):
    w_first = weights[0].reshape(9 * CHANNELS, CHANNELS)
    second_weight = weights[1].reshape(9 * CHANNELS, CHANNELS)
    learner_group = N_DP * N_SECTION
    global_row = (replay_owner * REPLAY_DEV + replay_slot).astype(jnp.int32).reshape(learner_group, BATCH_DEV)
    actions = sample_actions.reshape(learner_group, BATCH_DEV, SAMPLES)
    row_scale = jnp.full((BATCH_DEV,), 1.0 / LEARN_ROWS, jnp.float32)

    def visit(carry, item):
        row_index, learner_actions = item
        features = jnp.take(replay_rows, row_index, axis=0)
        move_return_estimates = jnp.take(qvalues, row_index, axis=0)
        reference_policy_entries = jnp.take(target_logits, row_index, axis=0)
        grad_first, grad_second = layer_grads(features, move_return_estimates, reference_policy_entries, learner_actions, row_scale, w_first, second_weight, head)
        return ((carry[0] + grad_first, carry[1] + grad_second), None)
    zeros = jnp.zeros((9 * CHANNELS, CHANNELS), jnp.float32)
    totals, _ = lax.scan(visit, (zeros, zeros), (global_row, actions))
    loss_derivative = jnp.stack([totals[0].reshape(-1), totals[1].reshape(-1)])
    first = beta_first * moment_first + (1.0 - beta_first) * loss_derivative
    second = beta_second * moment_second + (1.0 - beta_second) * loss_derivative * loss_derivative
    adam_step = first / (jnp.sqrt(second) + epsilon)
    new_weights = (master - learn_rate * adam_step).astype(jnp.bfloat16)
    return (adam_step, new_weights)
```

```python
import jax
import jax.numpy as jnp
from jax import lax
from jax.sharding import PartitionSpec as P

constant_entropy_scale = 0.5
trust_weight = 0.5
beta_first = 0.9
beta_second = 0.999
epsilon = 1e-08
learn_rate = 0.0001


def tap_stack(field):
    grid_side = field.shape[1]
    padded_rows = jnp.pad(field, ((0, 0), (1, 1), (1, 1), (0, 0)))
    return jnp.concatenate(
        [
            padded_rows[:, shift_row : shift_row + grid_side, shift_col : shift_col + grid_side, :]
            for shift_row in range(3)
            for shift_col in range(3)
        ],
        axis=-1,
    )


def layer_grads(
    features,
    move_return_estimates,
    reference_policy_entries,
    actions,
    row_scale,
    w_first,
    second_weight,
    head,
):
    row_count, grid_side, _, channels = features.shape
    positions = row_count * grid_side * grid_side
    taps_first = tap_stack(features).reshape(positions, 9 * channels)
    hidden = jax.nn.relu(jnp.dot(taps_first, w_first, preferred_element_type=jnp.float32)).astype(
        jnp.bfloat16
    )
    taps_second = tap_stack(hidden.reshape(features.shape)).reshape(positions, 9 * channels)
    summed = features.reshape(positions, channels).astype(jnp.float32) + jnp.dot(
        taps_second, second_weight, preferred_element_type=jnp.float32
    )
    block_out = jax.nn.relu(summed).astype(jnp.bfloat16)
    averaged_embedding = jnp.mean(
        block_out.astype(jnp.float32).reshape(row_count, grid_side * grid_side, channels), axis=1
    ).astype(jnp.bfloat16)
    logits = reference_policy_entries.astype(jnp.float32) + jnp.dot(
        averaged_embedding, head, preferred_element_type=jnp.float32
    )
    policy = jax.nn.softmax(logits, axis=-1)
    prior = jax.nn.softmax(reference_policy_entries.astype(jnp.float32), axis=-1)
    selected_moves = (actions[:, :, None] == jnp.arange(head.shape[1])[None, None, :]).astype(
        jnp.float32
    )
    move_logit_matrix = (
        jnp.einsum("vlu,vu->vl", selected_moves, move_return_estimates.astype(jnp.float32))
        / constant_entropy_scale
    )
    sample_weight = jax.nn.softmax(move_logit_matrix, axis=-1)
    logit_grad = (
        (1.0 + trust_weight) * policy
        - jnp.einsum("nk,nka->na", sample_weight, selected_moves)
        - trust_weight * prior
    ) * row_scale[:, None]
    pooled_grad = jnp.dot(logit_grad, head.astype(jnp.float32).T, precision=lax.Precision.HIGHEST)
    spread = jnp.broadcast_to(
        (pooled_grad / (grid_side * grid_side))[:, None, :],
        (row_count, grid_side * grid_side, channels),
    ).reshape(positions, channels)
    out_grad = jnp.where(block_out > 0, spread, 0.0).astype(jnp.bfloat16)
    grad_second = lax.dot_general(
        taps_second, out_grad, (((0,), (0,)), ((), ())), preferred_element_type=jnp.float32
    )
    flipped = (
        second_weight.reshape(9, channels, channels)[::-1]
        .transpose(0, 2, 1)
        .reshape(9 * channels, channels)
    )
    taps_back = tap_stack(out_grad.reshape(features.shape)).reshape(positions, 9 * channels)
    hidden_grad = jnp.where(
        hidden > 0, jnp.dot(taps_back, flipped, preferred_element_type=jnp.float32), 0.0
    ).astype(jnp.bfloat16)
    grad_first = lax.dot_general(
        taps_first, hidden_grad, (((0,), (0,)), ((), ())), preferred_element_type=jnp.float32
    )
    return (grad_first, grad_second)


def per_device(
    replay_rows,
    qvalues,
    target_logits,
    replay_owner,
    replay_slot,
    sample_actions,
    weights,
    head,
    master,
    moment_first,
    moment_second,
):
    rows_dev = replay_owner.shape[0]
    owners = lax.axis_size("dp")
    capacity = 2 * rows_dev // owners
    learn_rows = rows_dev * owners * lax.axis_size("section")
    channels = replay_rows.shape[3]
    w_first = weights[0].reshape(9 * channels, channels)
    second_weight = weights[1].reshape(9 * channels, channels)
    row_order = jnp.arange(rows_dev, dtype=jnp.int32)
    earlier = (replay_owner[None, :] == replay_owner[:, None]) & (
        row_order[None, :] < row_order[:, None]
    )
    rank_within = jnp.sum(earlier.astype(jnp.int32), axis=1)
    slot_index = replay_owner * capacity + rank_within
    matches = slot_index[None, :] == jnp.arange(owners * capacity, dtype=jnp.int32)[:, None]
    occupied_entries = jnp.any(matches, axis=1)
    source = jnp.sum(jnp.where(matches, row_order[None, :], 0), axis=1)
    request = jnp.where(occupied_entries, jnp.take(replay_slot, source), -1).reshape(
        owners, capacity
    )
    row_index = jnp.maximum(
        lax.all_to_all(request, "dp", split_axis=0, concat_axis=0, tiled=True), 0
    )
    feature_slots = lax.all_to_all(
        jnp.take(replay_rows, row_index, axis=0), "dp", split_axis=0, concat_axis=0, tiled=True
    )
    qvalue_slots = lax.all_to_all(
        jnp.take(qvalues, row_index, axis=0), "dp", split_axis=0, concat_axis=0, tiled=True
    )
    prior_slots = lax.all_to_all(
        jnp.take(target_logits, row_index, axis=0), "dp", split_axis=0, concat_axis=0, tiled=True
    )
    features = jnp.take(
        feature_slots.reshape((owners * capacity,) + feature_slots.shape[2:]), slot_index, axis=0
    )
    move_return_estimates = jnp.take(
        qvalue_slots.reshape(owners * capacity, -1), slot_index, axis=0
    )
    reference_policy_entries = jnp.take(
        prior_slots.reshape(owners * capacity, -1), slot_index, axis=0
    )
    row_scale = jnp.full((rows_dev,), 1.0 / learn_rows, jnp.float32)
    grad_first, grad_second = layer_grads(
        features,
        move_return_estimates,
        reference_policy_entries,
        sample_actions,
        row_scale,
        w_first,
        second_weight,
        head,
    )
    loss_derivative = jnp.stack([grad_first.reshape(-1), grad_second.reshape(-1)])
    piece_len = loss_derivative.shape[1] // owners
    layer = lax.axis_index("section")
    offset = lax.axis_index("dp") * piece_len
    summed = lax.psum(loss_derivative, ("dp", "section"))
    owned_grad = lax.dynamic_slice(summed, (layer, offset), (1, piece_len))
    first = beta_first * moment_first + (1.0 - beta_first) * owned_grad
    second = beta_second * moment_second + (1.0 - beta_second) * owned_grad * owned_grad
    adam_step = first / (jnp.sqrt(second) + epsilon)
    new_piece = (master - learn_rate * adam_step).astype(jnp.bfloat16).astype(jnp.float32)
    placed = lax.dynamic_update_slice(
        jnp.zeros(loss_derivative.shape, jnp.float32), new_piece, (layer, offset)
    )
    new_weights = lax.psum(placed, ("dp", "section")).astype(jnp.bfloat16)
    return (adam_step, new_weights)


def solution(mesh):
    placed = (
        P("dp", None, None, None),
        P("dp", None),
        P("dp", None),
        P(("dp", "section")),
        P(("dp", "section")),
        P(("dp", "section"), None),
        P(),
        P(),
        P("section", "dp"),
        P("section", "dp"),
        P("section", "dp"),
    )
    return jax.shard_map(
        per_device, mesh=mesh, in_specs=placed, out_specs=(P("section", "dp"), P()), check_vma=False
    )
```

```python
import jax
import jax.numpy as jnp
from jax import lax
from jax.sharding import PartitionSpec as P

constant_entropy_scale = 0.5
trust_weight = 0.5
beta_first = 0.9
beta_second = 0.999
epsilon = 1e-08
learn_rate = 0.0001


def tap_stack(field):
    grid_side = field.shape[1]
    padded_rows = jnp.pad(field, ((0, 0), (1, 1), (1, 1), (0, 0)))
    return jnp.concatenate(
        [
            padded_rows[:, shift_row : shift_row + grid_side, shift_col : shift_col + grid_side, :]
            for shift_row in range(3)
            for shift_col in range(3)
        ],
        axis=-1,
    )


def layer_grads(
    features,
    move_return_estimates,
    reference_policy_entries,
    actions,
    row_scale,
    w_first,
    second_weight,
    head,
):
    row_count, grid_side, _, channels = features.shape
    positions = row_count * grid_side * grid_side
    taps_first = tap_stack(features).reshape(positions, 9 * channels)
    hidden = jax.nn.relu(jnp.dot(taps_first, w_first, preferred_element_type=jnp.float32)).astype(
        jnp.bfloat16
    )
    taps_second = tap_stack(hidden.reshape(features.shape)).reshape(positions, 9 * channels)
    summed = features.reshape(positions, channels).astype(jnp.float32) + jnp.dot(
        taps_second, second_weight, preferred_element_type=jnp.float32
    )
    block_out = jax.nn.relu(summed).astype(jnp.bfloat16)
    averaged_embedding = jnp.mean(
        block_out.astype(jnp.float32).reshape(row_count, grid_side * grid_side, channels), axis=1
    ).astype(jnp.bfloat16)
    logits = reference_policy_entries.astype(jnp.float32) + jnp.dot(
        averaged_embedding, head, preferred_element_type=jnp.float32
    )
    policy = jax.nn.softmax(logits, axis=-1)
    prior = jax.nn.softmax(reference_policy_entries.astype(jnp.float32), axis=-1)
    selected_moves = (actions[:, :, None] == jnp.arange(head.shape[1])[None, None, :]).astype(
        jnp.float32
    )
    move_logit_matrix = (
        jnp.einsum("vlu,vu->vl", selected_moves, move_return_estimates.astype(jnp.float32))
        / constant_entropy_scale
    )
    sample_weight = jax.nn.softmax(move_logit_matrix, axis=-1)
    logit_grad = (
        (1.0 + trust_weight) * policy
        - jnp.einsum("nk,nka->na", sample_weight, selected_moves)
        - trust_weight * prior
    ) * row_scale[:, None]
    pooled_grad = jnp.dot(logit_grad, head.astype(jnp.float32).T, precision=lax.Precision.HIGHEST)
    spread = jnp.broadcast_to(
        (pooled_grad / (grid_side * grid_side))[:, None, :],
        (row_count, grid_side * grid_side, channels),
    ).reshape(positions, channels)
    out_grad = jnp.where(block_out > 0, spread, 0.0).astype(jnp.bfloat16)
    grad_second = lax.dot_general(
        taps_second, out_grad, (((0,), (0,)), ((), ())), preferred_element_type=jnp.float32
    )
    flipped = (
        second_weight.reshape(9, channels, channels)[::-1]
        .transpose(0, 2, 1)
        .reshape(9 * channels, channels)
    )
    taps_back = tap_stack(out_grad.reshape(features.shape)).reshape(positions, 9 * channels)
    hidden_grad = jnp.where(
        hidden > 0, jnp.dot(taps_back, flipped, preferred_element_type=jnp.float32), 0.0
    ).astype(jnp.bfloat16)
    grad_first = lax.dot_general(
        taps_first, hidden_grad, (((0,), (0,)), ((), ())), preferred_element_type=jnp.float32
    )
    return (grad_first, grad_second)


def per_device(
    replay_rows,
    qvalues,
    target_logits,
    replay_owner,
    replay_slot,
    sample_actions,
    weights,
    head,
    master,
    moment_first,
    moment_second,
):
    rows_dev = replay_owner.shape[0]
    owners = lax.axis_size("dp")
    capacity = 2 * rows_dev // owners
    learn_rows = rows_dev * owners * lax.axis_size("section")
    channels = replay_rows.shape[3]
    w_first = weights[0].reshape(9 * channels, channels)
    second_weight = weights[1].reshape(9 * channels, channels)
    row_order = jnp.arange(rows_dev, dtype=jnp.int32)
    earlier = (replay_owner[None, :] == replay_owner[:, None]) & (
        row_order[None, :] < row_order[:, None]
    )
    rank_within = jnp.sum(earlier.astype(jnp.int32), axis=1)
    slot_index = replay_owner * capacity + rank_within
    matches = slot_index[None, :] == jnp.arange(owners * capacity, dtype=jnp.int32)[:, None]
    occupied_entries = jnp.any(matches, axis=1)
    source = jnp.sum(jnp.where(matches, row_order[None, :], 0), axis=1)
    request = jnp.where(occupied_entries, jnp.take(replay_slot, source), -1).reshape(
        owners, capacity
    )
    row_index = jnp.maximum(
        lax.all_to_all(request, "dp", split_axis=0, concat_axis=0, tiled=True), 0
    )
    feature_slots = lax.all_to_all(
        jnp.take(replay_rows, row_index, axis=0), "dp", split_axis=0, concat_axis=0, tiled=True
    )
    qvalue_slots = lax.all_to_all(
        jnp.take(qvalues, row_index, axis=0), "dp", split_axis=0, concat_axis=0, tiled=True
    )
    prior_slots = lax.all_to_all(
        jnp.take(target_logits, row_index, axis=0), "dp", split_axis=0, concat_axis=0, tiled=True
    )
    features = jnp.take(
        feature_slots.reshape((owners * capacity,) + feature_slots.shape[2:]), slot_index, axis=0
    )
    move_return_estimates = jnp.take(
        qvalue_slots.reshape(owners * capacity, -1), slot_index, axis=0
    )
    reference_policy_entries = jnp.take(
        prior_slots.reshape(owners * capacity, -1), slot_index, axis=0
    )
    row_scale = jnp.full((rows_dev,), 1.0 / learn_rows, jnp.float32)
    grad_first, grad_second = layer_grads(
        features,
        move_return_estimates,
        reference_policy_entries,
        sample_actions,
        row_scale,
        w_first,
        second_weight,
        head,
    )
    loss_derivative = jnp.stack([grad_first.reshape(-1), grad_second.reshape(-1)])
    piece_len = loss_derivative.shape[1] // owners
    regrouped = (
        loss_derivative.reshape(2, owners, piece_len)
        .transpose(1, 0, 2)
        .reshape(2 * owners, piece_len)
    )
    contributions = lax.all_to_all(
        regrouped, ("dp", "section"), split_axis=0, concat_axis=0, tiled=True
    )
    owned_grad = jnp.sum(contributions, axis=0, keepdims=True)
    first = beta_first * moment_first + (1.0 - beta_first) * owned_grad
    second = beta_second * moment_second + (1.0 - beta_second) * owned_grad * owned_grad
    adam_step = first / (jnp.sqrt(second) + epsilon)
    new_piece = (master - learn_rate * adam_step).astype(jnp.bfloat16)
    collected = lax.all_to_all(
        jnp.broadcast_to(new_piece, (2 * owners, piece_len)),
        ("dp", "section"),
        split_axis=0,
        concat_axis=0,
        tiled=True,
    )
    new_weights = (
        collected.reshape(owners, 2, piece_len).transpose(1, 0, 2).reshape(2, owners * piece_len)
    )
    return (adam_step, new_weights)


def solution(mesh):
    placed = (
        P("dp", None, None, None),
        P("dp", None),
        P("dp", None),
        P(("dp", "section")),
        P(("dp", "section")),
        P(("dp", "section"), None),
        P(),
        P(),
        P("section", "dp"),
        P("section", "dp"),
        P("section", "dp"),
    )
    return jax.shard_map(
        per_device, mesh=mesh, in_specs=placed, out_specs=(P("section", "dp"), P()), check_vma=False
    )
```

```python
import jax
import jax.numpy as jnp
from jax import lax
from jax.sharding import PartitionSpec as P

constant_entropy_scale = 0.5
trust_weight = 0.5
beta_first = 0.9
beta_second = 0.999
epsilon = 1e-08
learn_rate = 0.0001


def tap_stack(field):
    grid_side = field.shape[1]
    padded_rows = jnp.pad(field, ((0, 0), (1, 1), (1, 1), (0, 0)))
    return jnp.concatenate(
        [
            padded_rows[:, shift_row : shift_row + grid_side, shift_col : shift_col + grid_side, :]
            for shift_row in range(3)
            for shift_col in range(3)
        ],
        axis=-1,
    )


def layer_grads(
    features,
    move_return_estimates,
    reference_policy_entries,
    actions,
    row_scale,
    w_first,
    second_weight,
    head,
):
    row_count, grid_side, _, channels = features.shape
    positions = row_count * grid_side * grid_side
    taps_first = tap_stack(features).reshape(positions, 9 * channels)
    hidden = jax.nn.relu(jnp.dot(taps_first, w_first, preferred_element_type=jnp.float32)).astype(
        jnp.bfloat16
    )
    taps_second = tap_stack(hidden.reshape(features.shape)).reshape(positions, 9 * channels)
    summed = features.reshape(positions, channels).astype(jnp.float32) + jnp.dot(
        taps_second, second_weight, preferred_element_type=jnp.float32
    )
    block_out = jax.nn.relu(summed).astype(jnp.bfloat16)
    averaged_embedding = jnp.mean(
        block_out.astype(jnp.float32).reshape(row_count, grid_side * grid_side, channels), axis=1
    ).astype(jnp.bfloat16)
    logits = reference_policy_entries.astype(jnp.float32) + jnp.dot(
        averaged_embedding, head, preferred_element_type=jnp.float32
    )
    policy = jax.nn.softmax(logits, axis=-1)
    prior = jax.nn.softmax(reference_policy_entries.astype(jnp.float32), axis=-1)
    selected_moves = (actions[:, :, None] == jnp.arange(head.shape[1])[None, None, :]).astype(
        jnp.float32
    )
    move_logit_matrix = (
        jnp.einsum("vlu,vu->vl", selected_moves, move_return_estimates.astype(jnp.float32))
        / constant_entropy_scale
    )
    sample_weight = jax.nn.softmax(move_logit_matrix, axis=-1)
    logit_grad = (
        (1.0 + trust_weight) * policy
        - jnp.einsum("nk,nka->na", sample_weight, selected_moves)
        - trust_weight * prior
    ) * row_scale[:, None]
    pooled_grad = jnp.dot(logit_grad, head.astype(jnp.float32).T, precision=lax.Precision.HIGHEST)
    spread = jnp.broadcast_to(
        (pooled_grad / (grid_side * grid_side))[:, None, :],
        (row_count, grid_side * grid_side, channels),
    ).reshape(positions, channels)
    out_grad = jnp.where(block_out > 0, spread, 0.0).astype(jnp.bfloat16)
    grad_second = lax.dot_general(
        taps_second, out_grad, (((0,), (0,)), ((), ())), preferred_element_type=jnp.float32
    )
    flipped = (
        second_weight.reshape(9, channels, channels)[::-1]
        .transpose(0, 2, 1)
        .reshape(9 * channels, channels)
    )
    taps_back = tap_stack(out_grad.reshape(features.shape)).reshape(positions, 9 * channels)
    hidden_grad = jnp.where(
        hidden > 0, jnp.dot(taps_back, flipped, preferred_element_type=jnp.float32), 0.0
    ).astype(jnp.bfloat16)
    grad_first = lax.dot_general(
        taps_first, hidden_grad, (((0,), (0,)), ((), ())), preferred_element_type=jnp.float32
    )
    return (grad_first, grad_second)


def per_device(
    replay_rows,
    qvalues,
    target_logits,
    replay_owner,
    replay_slot,
    sample_actions,
    weights,
    head,
    master,
    moment_first,
    moment_second,
):
    rows_dev = replay_owner.shape[0]
    owners = lax.axis_size("dp")
    capacity = 2 * rows_dev // owners
    learn_rows = rows_dev * owners * lax.axis_size("section")
    channels = replay_rows.shape[3]
    w_first = weights[0].reshape(9 * channels, channels)
    second_weight = weights[1].reshape(9 * channels, channels)
    row_order = jnp.arange(rows_dev, dtype=jnp.int32)
    earlier = (replay_owner[None, :] == replay_owner[:, None]) & (
        row_order[None, :] < row_order[:, None]
    )
    rank_within = jnp.sum(earlier.astype(jnp.int32), axis=1)
    slot_index = replay_owner * capacity + rank_within
    matches = slot_index[None, :] == jnp.arange(owners * capacity, dtype=jnp.int32)[:, None]
    occupied_entries = jnp.any(matches, axis=1)
    source = jnp.sum(jnp.where(matches, row_order[None, :], 0), axis=1)
    request = jnp.where(occupied_entries, jnp.take(replay_slot, source), -1).reshape(
        owners, capacity
    )
    row_index = jnp.maximum(
        lax.all_to_all(request, "dp", split_axis=0, concat_axis=0, tiled=True), 0
    )
    row_width = replay_rows.shape[1] * replay_rows.shape[2] * channels
    actions_n = qvalues.shape[1]
    packed = jnp.concatenate(
        [
            jnp.take(replay_rows.reshape(-1, row_width), row_index, axis=0),
            jnp.take(qvalues, row_index, axis=0),
            jnp.take(target_logits, row_index, axis=0),
        ],
        axis=-1,
    )
    slots = lax.all_to_all(packed, "dp", split_axis=0, concat_axis=0, tiled=True)
    picked = jnp.take(slots.reshape(owners * capacity, -1), slot_index, axis=0)
    features = picked[:, :row_width].reshape((rows_dev,) + replay_rows.shape[1:])
    move_return_estimates = picked[:, row_width : row_width + actions_n]
    reference_policy_entries = picked[:, row_width + actions_n :]
    row_scale = jnp.full((rows_dev,), 1.0 / learn_rows, jnp.float32)
    grad_first, grad_second = layer_grads(
        features,
        move_return_estimates,
        reference_policy_entries,
        sample_actions,
        row_scale,
        w_first,
        second_weight,
        head,
    )
    loss_derivative = jnp.stack([grad_first.reshape(-1), grad_second.reshape(-1)])
    piece_len = loss_derivative.shape[1] // owners
    layer = lax.axis_index("section")
    swap = [(0, 1), (1, 0)]
    contributions = lax.all_to_all(
        loss_derivative.reshape(2, owners, piece_len).transpose(1, 0, 2),
        "dp",
        split_axis=0,
        concat_axis=0,
        tiled=True,
    )
    partial = jnp.sum(contributions, axis=0)
    from_partner = lax.ppermute(
        lax.dynamic_slice_in_dim(partial, 1 - layer, 1, axis=0), "section", swap
    )
    owned_grad = lax.dynamic_slice_in_dim(partial, layer, 1, axis=0) + from_partner
    first = beta_first * moment_first + (1.0 - beta_first) * owned_grad
    second = beta_second * moment_second + (1.0 - beta_second) * owned_grad * owned_grad
    adam_step = first / (jnp.sqrt(second) + epsilon)
    new_piece = (master - learn_rate * adam_step).astype(jnp.bfloat16)
    partner_piece = lax.ppermute(new_piece, "section", swap)
    both_layers = jnp.where(
        layer == 0,
        jnp.concatenate([new_piece, partner_piece]),
        jnp.concatenate([partner_piece, new_piece]),
    )
    collected = lax.all_to_all(
        jnp.broadcast_to(both_layers[None], (owners, 2, piece_len)),
        "dp",
        split_axis=0,
        concat_axis=0,
        tiled=True,
    )
    new_weights = collected.transpose(1, 0, 2).reshape(2, owners * piece_len)
    return (adam_step, new_weights)


def solution(mesh):
    placed = (
        P("dp", None, None, None),
        P("dp", None),
        P("dp", None),
        P(("dp", "section")),
        P(("dp", "section")),
        P(("dp", "section"), None),
        P(),
        P(),
        P("section", "dp"),
        P("section", "dp"),
        P("section", "dp"),
    )
    return jax.shard_map(
        per_device, mesh=mesh, in_specs=placed, out_specs=(P("section", "dp"), P()), check_vma=False
    )
```

```python
import jax
import jax.numpy as jnp
from jax import lax
from jax.sharding import PartitionSpec as P

constant_entropy_scale = 0.5
trust_weight = 0.5
beta_first = 0.9
beta_second = 0.999
epsilon = 1e-08
learn_rate = 0.0001


def tap_stack(field):
    grid_side = field.shape[1]
    padded_rows = jnp.pad(field, ((0, 0), (1, 1), (1, 1), (0, 0)))
    return jnp.concatenate(
        [
            padded_rows[:, shift_row : shift_row + grid_side, shift_col : shift_col + grid_side, :]
            for shift_row in range(3)
            for shift_col in range(3)
        ],
        axis=-1,
    )


def layer_grads(
    features,
    move_return_estimates,
    reference_policy_entries,
    actions,
    row_scale,
    w_first,
    second_weight,
    head,
):
    row_count, grid_side, _, channels = features.shape
    positions = row_count * grid_side * grid_side
    taps_first = tap_stack(features).reshape(positions, 9 * channels)
    hidden = jax.nn.relu(jnp.dot(taps_first, w_first, preferred_element_type=jnp.float32)).astype(
        jnp.bfloat16
    )
    taps_second = tap_stack(hidden.reshape(features.shape)).reshape(positions, 9 * channels)
    summed = features.reshape(positions, channels).astype(jnp.float32) + jnp.dot(
        taps_second, second_weight, preferred_element_type=jnp.float32
    )
    block_out = jax.nn.relu(summed).astype(jnp.bfloat16)
    averaged_embedding = jnp.mean(
        block_out.astype(jnp.float32).reshape(row_count, grid_side * grid_side, channels), axis=1
    ).astype(jnp.bfloat16)
    logits = reference_policy_entries.astype(jnp.float32) + jnp.dot(
        averaged_embedding, head, preferred_element_type=jnp.float32
    )
    policy = jax.nn.softmax(logits, axis=-1)
    prior = jax.nn.softmax(reference_policy_entries.astype(jnp.float32), axis=-1)
    selected_moves = (actions[:, :, None] == jnp.arange(head.shape[1])[None, None, :]).astype(
        jnp.float32
    )
    move_logit_matrix = (
        jnp.einsum("vlu,vu->vl", selected_moves, move_return_estimates.astype(jnp.float32))
        / constant_entropy_scale
    )
    sample_weight = jax.nn.softmax(move_logit_matrix, axis=-1)
    logit_grad = (
        (1.0 + trust_weight) * policy
        - jnp.einsum("nk,nka->na", sample_weight, selected_moves)
        - trust_weight * prior
    ) * row_scale[:, None]
    pooled_grad = jnp.dot(logit_grad, head.astype(jnp.float32).T, precision=lax.Precision.HIGHEST)
    spread = jnp.broadcast_to(
        (pooled_grad / (grid_side * grid_side))[:, None, :],
        (row_count, grid_side * grid_side, channels),
    ).reshape(positions, channels)
    out_grad = jnp.where(block_out > 0, spread, 0.0).astype(jnp.bfloat16)
    grad_second = lax.dot_general(
        taps_second, out_grad, (((0,), (0,)), ((), ())), preferred_element_type=jnp.float32
    )
    flipped = (
        second_weight.reshape(9, channels, channels)[::-1]
        .transpose(0, 2, 1)
        .reshape(9 * channels, channels)
    )
    taps_back = tap_stack(out_grad.reshape(features.shape)).reshape(positions, 9 * channels)
    hidden_grad = jnp.where(
        hidden > 0, jnp.dot(taps_back, flipped, preferred_element_type=jnp.float32), 0.0
    ).astype(jnp.bfloat16)
    grad_first = lax.dot_general(
        taps_first, hidden_grad, (((0,), (0,)), ((), ())), preferred_element_type=jnp.float32
    )
    return (grad_first, grad_second)


def per_device(
    replay_rows,
    qvalues,
    target_logits,
    replay_owner,
    replay_slot,
    sample_actions,
    weights,
    head,
    master,
    moment_first,
    moment_second,
):
    rows_dev = replay_owner.shape[0]
    owners = lax.axis_size("dp")
    capacity = 2 * rows_dev // owners
    learn_rows = rows_dev * owners * lax.axis_size("section")
    channels = replay_rows.shape[3]
    w_first = weights[0].reshape(9 * channels, channels)
    second_weight = weights[1].reshape(9 * channels, channels)
    layer = lax.axis_index("section")
    swap = [(0, 1), (1, 0)]
    own_state = jnp.concatenate([master, moment_first, moment_second])
    partner_state = lax.ppermute(own_state, "section", swap)
    state = jnp.where(
        layer == 0,
        jnp.stack([own_state, partner_state], axis=1),
        jnp.stack([partner_state, own_state], axis=1),
    )
    row_order = jnp.arange(rows_dev, dtype=jnp.int32)
    earlier = (replay_owner[None, :] == replay_owner[:, None]) & (
        row_order[None, :] < row_order[:, None]
    )
    rank_within = jnp.sum(earlier.astype(jnp.int32), axis=1)
    slot_index = replay_owner * capacity + rank_within
    matches = slot_index[None, :] == jnp.arange(owners * capacity, dtype=jnp.int32)[:, None]
    occupied_entries = jnp.any(matches, axis=1)
    source = jnp.sum(jnp.where(matches, row_order[None, :], 0), axis=1)
    request = jnp.where(occupied_entries, jnp.take(replay_slot, source), -1).reshape(
        owners, capacity
    )
    row_index = jnp.maximum(
        lax.all_to_all(request, "dp", split_axis=0, concat_axis=0, tiled=True), 0
    )
    row_width = replay_rows.shape[1] * replay_rows.shape[2] * channels
    actions_n = qvalues.shape[1]
    packed = jnp.concatenate(
        [
            jnp.take(replay_rows.reshape(-1, row_width), row_index, axis=0),
            jnp.take(qvalues, row_index, axis=0),
            jnp.take(target_logits, row_index, axis=0),
        ],
        axis=-1,
    )
    slots = lax.all_to_all(packed, "dp", split_axis=0, concat_axis=0, tiled=True)
    picked = jnp.take(slots.reshape(owners * capacity, -1), slot_index, axis=0)
    features = picked[:, :row_width].reshape((rows_dev,) + replay_rows.shape[1:])
    move_return_estimates = picked[:, row_width : row_width + actions_n]
    reference_policy_entries = picked[:, row_width + actions_n :]
    row_scale = jnp.full((rows_dev,), 1.0 / learn_rows, jnp.float32)
    grad_first, grad_second = layer_grads(
        features,
        move_return_estimates,
        reference_policy_entries,
        sample_actions,
        row_scale,
        w_first,
        second_weight,
        head,
    )
    loss_derivative = jnp.stack([grad_first.reshape(-1), grad_second.reshape(-1)])
    piece_len = loss_derivative.shape[1] // owners
    contributions = lax.all_to_all(
        loss_derivative.reshape(2, owners, piece_len).transpose(1, 0, 2),
        "dp",
        split_axis=0,
        concat_axis=0,
        tiled=True,
    )
    partial = jnp.sum(contributions, axis=0)
    owned_grad = partial + lax.ppermute(partial, "section", swap)
    first = beta_first * state[1] + (1.0 - beta_first) * owned_grad
    second = beta_second * state[2] + (1.0 - beta_second) * owned_grad * owned_grad
    both_steps = first / (jnp.sqrt(second) + epsilon)
    both_layers = (state[0] - learn_rate * both_steps).astype(jnp.bfloat16)
    adam_step = lax.dynamic_slice_in_dim(both_steps, layer, 1, axis=0)
    collected = lax.all_to_all(
        jnp.broadcast_to(both_layers[None], (owners, 2, piece_len)),
        "dp",
        split_axis=0,
        concat_axis=0,
        tiled=True,
    )
    new_weights = collected.transpose(1, 0, 2).reshape(2, owners * piece_len)
    return (adam_step, new_weights)


def solution(mesh):
    placed = (
        P("dp", None, None, None),
        P("dp", None),
        P("dp", None),
        P(("dp", "section")),
        P(("dp", "section")),
        P(("dp", "section"), None),
        P(),
        P(),
        P("section", "dp"),
        P("section", "dp"),
        P("section", "dp"),
    )
    return jax.shard_map(
        per_device, mesh=mesh, in_specs=placed, out_specs=(P("section", "dp"), P()), check_vma=False
    )
```

```python
import jax
import jax.numpy as jnp
from jax import lax
from jax.sharding import PartitionSpec as P

constant_entropy_scale = 0.5
trust_weight = 0.5
beta_first = 0.9
beta_second = 0.999
epsilon = 1e-08
learn_rate = 0.0001


def tap_stack(field):
    grid_side = field.shape[1]
    padded_rows = jnp.pad(field, ((0, 0), (1, 1), (1, 1), (0, 0)))
    return jnp.concatenate(
        [
            padded_rows[:, shift_row : shift_row + grid_side, shift_col : shift_col + grid_side, :]
            for shift_row in range(3)
            for shift_col in range(3)
        ],
        axis=-1,
    )


def conv_taps(field, kernel):
    channels = field.shape[3]
    return lax.conv_general_dilated(
        field,
        kernel.reshape(3, 3, channels, -1),
        (1, 1),
        ((1, 1), (1, 1)),
        dimension_numbers=("NHWC", "HWIO", "NHWC"),
        preferred_element_type=jnp.float32,
    )


def conv_kernel_grad(field, out_grad):
    numbers = lax.ConvDimensionNumbers(
        lhs_spec=(3, 0, 1, 2), rhs_spec=(3, 0, 1, 2), out_spec=(2, 3, 0, 1)
    )
    grad = lax.conv_general_dilated(
        field,
        out_grad,
        (1, 1),
        ((1, 1), (1, 1)),
        dimension_numbers=numbers,
        preferred_element_type=jnp.float32,
    )
    return grad.reshape(9 * field.shape[3], out_grad.shape[3])


def layer_grads(
    features,
    move_return_estimates,
    reference_policy_entries,
    actions,
    row_scale,
    w_first,
    second_weight,
    head,
):
    row_count, grid_side, _, channels = features.shape
    positions = row_count * grid_side * grid_side
    hidden = jax.nn.relu(conv_taps(features, w_first)).astype(jnp.bfloat16)
    summed = features.reshape(positions, channels).astype(jnp.float32) + conv_taps(
        hidden, second_weight
    ).reshape(positions, channels)
    block_out = jax.nn.relu(summed).astype(jnp.bfloat16)
    averaged_embedding = jnp.mean(
        block_out.astype(jnp.float32).reshape(row_count, grid_side * grid_side, channels), axis=1
    ).astype(jnp.bfloat16)
    logits = reference_policy_entries.astype(jnp.float32) + jnp.dot(
        averaged_embedding, head, preferred_element_type=jnp.float32
    )
    policy = jax.nn.softmax(logits, axis=-1)
    prior = jax.nn.softmax(reference_policy_entries.astype(jnp.float32), axis=-1)
    selected_moves = (actions[:, :, None] == jnp.arange(head.shape[1])[None, None, :]).astype(
        jnp.float32
    )
    move_logit_matrix = (
        jnp.einsum("vlu,vu->vl", selected_moves, move_return_estimates.astype(jnp.float32))
        / constant_entropy_scale
    )
    sample_weight = jax.nn.softmax(move_logit_matrix, axis=-1)
    logit_grad = (
        (1.0 + trust_weight) * policy
        - jnp.einsum("nk,nka->na", sample_weight, selected_moves)
        - trust_weight * prior
    ) * row_scale[:, None]
    pooled_grad = jnp.dot(logit_grad, head.astype(jnp.float32).T, precision=lax.Precision.HIGHEST)
    spread = jnp.broadcast_to(
        (pooled_grad / (grid_side * grid_side))[:, None, :],
        (row_count, grid_side * grid_side, channels),
    ).reshape(positions, channels)
    out_grad = jnp.where(block_out > 0, spread, 0.0).astype(jnp.bfloat16)
    grad_second = conv_kernel_grad(hidden, out_grad.reshape(features.shape))
    flipped = (
        second_weight.reshape(9, channels, channels)[::-1]
        .transpose(0, 2, 1)
        .reshape(9 * channels, channels)
    )
    hidden_grad = jnp.where(
        hidden > 0, conv_taps(out_grad.reshape(features.shape), flipped), 0.0
    ).astype(jnp.bfloat16)
    grad_first = conv_kernel_grad(features, hidden_grad)
    return (grad_first, grad_second)


def per_device(
    replay_rows,
    qvalues,
    target_logits,
    replay_owner,
    replay_slot,
    sample_actions,
    weights,
    head,
    master,
    moment_first,
    moment_second,
):
    rows_dev = replay_owner.shape[0]
    owners = lax.axis_size("dp")
    capacity = 2 * rows_dev // owners
    learn_rows = rows_dev * owners * lax.axis_size("section")
    channels = replay_rows.shape[3]
    w_first = weights[0].reshape(9 * channels, channels)
    second_weight = weights[1].reshape(9 * channels, channels)
    layer = lax.axis_index("section")
    swap = [(0, 1), (1, 0)]
    own_state = jnp.concatenate([master, moment_first, moment_second])
    partner_state = lax.ppermute(own_state, "section", swap)
    state = jnp.where(
        layer == 0,
        jnp.stack([own_state, partner_state], axis=1),
        jnp.stack([partner_state, own_state], axis=1),
    )
    row_order = jnp.arange(rows_dev, dtype=jnp.int32)
    earlier = (replay_owner[None, :] == replay_owner[:, None]) & (
        row_order[None, :] < row_order[:, None]
    )
    rank_within = jnp.sum(earlier.astype(jnp.int32), axis=1)
    slot_index = replay_owner * capacity + rank_within
    matches = slot_index[None, :] == jnp.arange(owners * capacity, dtype=jnp.int32)[:, None]
    occupied_entries = jnp.any(matches, axis=1)
    source = jnp.sum(jnp.where(matches, row_order[None, :], 0), axis=1)
    request = jnp.where(occupied_entries, jnp.take(replay_slot, source), -1).reshape(
        owners, capacity
    )
    row_index = jnp.maximum(
        lax.all_to_all(request, "dp", split_axis=0, concat_axis=0, tiled=True), 0
    )
    row_width = replay_rows.shape[1] * replay_rows.shape[2] * channels
    actions_n = qvalues.shape[1]
    packed = jnp.concatenate(
        [
            jnp.take(replay_rows.reshape(-1, row_width), row_index, axis=0),
            jnp.take(qvalues, row_index, axis=0),
            jnp.take(target_logits, row_index, axis=0),
        ],
        axis=-1,
    )
    slots = lax.all_to_all(packed, "dp", split_axis=0, concat_axis=0, tiled=True)
    picked = jnp.take(slots.reshape(owners * capacity, -1), slot_index, axis=0)
    features = picked[:, :row_width].reshape((rows_dev,) + replay_rows.shape[1:])
    move_return_estimates = picked[:, row_width : row_width + actions_n]
    reference_policy_entries = picked[:, row_width + actions_n :]
    row_scale = jnp.full((rows_dev,), 1.0 / learn_rows, jnp.float32)
    grad_first, grad_second = layer_grads(
        features,
        move_return_estimates,
        reference_policy_entries,
        sample_actions,
        row_scale,
        w_first,
        second_weight,
        head,
    )
    loss_derivative = jnp.stack([grad_first.reshape(-1), grad_second.reshape(-1)])
    piece_len = loss_derivative.shape[1] // owners
    contributions = lax.all_to_all(
        loss_derivative.reshape(2, owners, piece_len).transpose(1, 0, 2),
        "dp",
        split_axis=0,
        concat_axis=0,
        tiled=True,
    )
    partial = jnp.sum(contributions, axis=0)
    owned_grad = partial + lax.ppermute(partial, "section", swap)
    first = beta_first * state[1] + (1.0 - beta_first) * owned_grad
    second = beta_second * state[2] + (1.0 - beta_second) * owned_grad * owned_grad
    both_steps = first / (jnp.sqrt(second) + epsilon)
    both_layers = (state[0] - learn_rate * both_steps).astype(jnp.bfloat16)
    adam_step = lax.dynamic_slice_in_dim(both_steps, layer, 1, axis=0)
    collected = lax.all_to_all(
        jnp.broadcast_to(both_layers[None], (owners, 2, piece_len)),
        "dp",
        split_axis=0,
        concat_axis=0,
        tiled=True,
    )
    new_weights = collected.transpose(1, 0, 2).reshape(2, owners * piece_len)
    return (adam_step, new_weights)


def solution(mesh):
    placed = (
        P("dp", None, None, None),
        P("dp", None),
        P("dp", None),
        P(("dp", "section")),
        P(("dp", "section")),
        P(("dp", "section"), None),
        P(),
        P(),
        P("section", "dp"),
        P("section", "dp"),
        P("section", "dp"),
    )
    return jax.shard_map(
        per_device, mesh=mesh, in_specs=placed, out_specs=(P("section", "dp"), P()), check_vma=False
    )
```

```python
import jax
import jax.numpy as jnp
from jax import lax
from jax.sharding import PartitionSpec as P

constant_entropy_scale = 0.5
trust_weight = 0.5
beta_first = 0.9
beta_second = 0.999
epsilon = 1e-08
learn_rate = 0.0001


def tap_stack(field):
    grid_side = field.shape[1]
    padded_rows = jnp.pad(field, ((0, 0), (1, 1), (1, 1), (0, 0)))
    return jnp.concatenate(
        [
            padded_rows[:, shift_row : shift_row + grid_side, shift_col : shift_col + grid_side, :]
            for shift_row in range(3)
            for shift_col in range(3)
        ],
        axis=-1,
    )


def conv_taps(field, kernel):
    channels = field.shape[3]
    return lax.conv_general_dilated(
        field,
        kernel.reshape(3, 3, channels, -1),
        (1, 1),
        ((1, 1), (1, 1)),
        dimension_numbers=("NHWC", "HWIO", "NHWC"),
        preferred_element_type=jnp.float32,
    )


def conv_kernel_grad(field, out_grad):
    numbers = lax.ConvDimensionNumbers(
        lhs_spec=(3, 0, 1, 2), rhs_spec=(3, 0, 1, 2), out_spec=(2, 3, 0, 1)
    )
    grad = lax.conv_general_dilated(
        field,
        out_grad,
        (1, 1),
        ((1, 1), (1, 1)),
        dimension_numbers=numbers,
        preferred_element_type=jnp.float32,
    )
    return grad.reshape(9 * field.shape[3], out_grad.shape[3])


def layer_grads(
    features,
    move_return_estimates,
    reference_policy_entries,
    actions,
    row_scale,
    w_first,
    second_weight,
    head,
):
    row_count, grid_side, _, channels = features.shape
    positions = row_count * grid_side * grid_side
    hidden = jax.nn.relu(conv_taps(features, w_first)).astype(jnp.bfloat16)
    summed = features.reshape(positions, channels).astype(jnp.float32) + conv_taps(
        hidden, second_weight
    ).reshape(positions, channels)
    block_out = jax.nn.relu(summed).astype(jnp.bfloat16)
    averaged_embedding = jnp.mean(
        block_out.astype(jnp.float32).reshape(row_count, grid_side * grid_side, channels), axis=1
    ).astype(jnp.bfloat16)
    logits = reference_policy_entries.astype(jnp.float32) + jnp.dot(
        averaged_embedding, head, preferred_element_type=jnp.float32
    )
    policy = jax.nn.softmax(logits, axis=-1)
    prior = jax.nn.softmax(reference_policy_entries.astype(jnp.float32), axis=-1)
    selected_moves = (actions[:, :, None] == jnp.arange(head.shape[1])[None, None, :]).astype(
        jnp.float32
    )
    move_logit_matrix = (
        jnp.einsum("vlu,vu->vl", selected_moves, move_return_estimates.astype(jnp.float32))
        / constant_entropy_scale
    )
    sample_weight = jax.nn.softmax(move_logit_matrix, axis=-1)
    logit_grad = (
        (1.0 + trust_weight) * policy
        - jnp.einsum("nk,nka->na", sample_weight, selected_moves)
        - trust_weight * prior
    ) * row_scale[:, None]
    pooled_grad = jnp.dot(logit_grad, head.astype(jnp.float32).T, precision=lax.Precision.HIGHEST)
    spread = jnp.broadcast_to(
        (pooled_grad / (grid_side * grid_side))[:, None, :],
        (row_count, grid_side * grid_side, channels),
    ).reshape(positions, channels)
    out_grad = jnp.where(block_out > 0, spread, 0.0).astype(jnp.bfloat16)
    grad_second = conv_kernel_grad(hidden, out_grad.reshape(features.shape))
    flipped = (
        second_weight.reshape(9, channels, channels)[::-1]
        .transpose(0, 2, 1)
        .reshape(9 * channels, channels)
    )
    hidden_grad = jnp.where(
        hidden > 0, conv_taps(out_grad.reshape(features.shape), flipped), 0.0
    ).astype(jnp.bfloat16)
    grad_first = conv_kernel_grad(features, hidden_grad)
    return (grad_first, grad_second)


def per_device(
    replay_rows,
    qvalues,
    target_logits,
    replay_owner,
    replay_slot,
    sample_actions,
    weights,
    head,
    master,
    moment_first,
    moment_second,
):
    rows_dev = replay_owner.shape[0]
    owners = lax.axis_size("dp")
    capacity = 2 * rows_dev // owners
    learn_rows = rows_dev * owners * lax.axis_size("section")
    channels = replay_rows.shape[3]
    w_first = weights[0].reshape(9 * channels, channels)
    second_weight = weights[1].reshape(9 * channels, channels)
    layer = lax.axis_index("section")
    swap = [(0, 1), (1, 0)]
    own_state = jnp.concatenate([master, moment_first, moment_second])
    partner_state = lax.ppermute(own_state, "section", swap)
    state = jnp.where(
        layer == 0,
        jnp.stack([own_state, partner_state], axis=1),
        jnp.stack([partner_state, own_state], axis=1),
    )
    row_order = jnp.arange(rows_dev, dtype=jnp.int32)
    earlier = (replay_owner[None, :] == replay_owner[:, None]) & (
        row_order[None, :] < row_order[:, None]
    )
    rank_within = jnp.sum(earlier.astype(jnp.int32), axis=1)
    slot_index = replay_owner * capacity + rank_within
    matches = slot_index[None, :] == jnp.arange(owners * capacity, dtype=jnp.int32)[:, None]
    occupied_entries = jnp.any(matches, axis=1)
    source = jnp.sum(jnp.where(matches, row_order[None, :], 0), axis=1)
    request = jnp.where(occupied_entries, jnp.take(replay_slot, source), -1).reshape(
        owners, capacity
    )
    row_index = jnp.maximum(
        lax.all_to_all(request, "dp", split_axis=0, concat_axis=0, tiled=True), 0
    )
    cells = replay_rows.shape[1] * replay_rows.shape[2]
    actions_n = qvalues.shape[1]
    side = jnp.concatenate(
        [
            jnp.take(qvalues, row_index, axis=0),
            jnp.take(target_logits, row_index, axis=0),
            jnp.zeros(row_index.shape + (channels - 2 * actions_n,), qvalues.dtype),
        ],
        axis=-1,
    )
    packed = jnp.concatenate(
        [
            jnp.take(replay_rows.reshape(-1, cells, channels), row_index, axis=0),
            side[:, :, None, :],
        ],
        axis=2,
    )
    slots = lax.all_to_all(packed, "dp", split_axis=0, concat_axis=0, tiled=True)
    picked = jnp.take(
        slots.reshape((owners * capacity,) + slots.shape[2:]), slot_index, axis=0
    )
    features = picked[:, :cells].reshape((rows_dev,) + replay_rows.shape[1:])
    move_return_estimates = picked[:, cells, :actions_n]
    reference_policy_entries = picked[:, cells, actions_n : 2 * actions_n]
    row_scale = jnp.full((rows_dev,), 1.0 / learn_rows, jnp.float32)
    grad_first, grad_second = layer_grads(
        features,
        move_return_estimates,
        reference_policy_entries,
        sample_actions,
        row_scale,
        w_first,
        second_weight,
        head,
    )
    loss_derivative = jnp.stack([grad_first.reshape(-1), grad_second.reshape(-1)])
    piece_len = loss_derivative.shape[1] // owners
    contributions = lax.all_to_all(
        loss_derivative.reshape(2, owners, piece_len).transpose(1, 0, 2),
        "dp",
        split_axis=0,
        concat_axis=0,
        tiled=True,
    )
    partial = jnp.sum(contributions, axis=0)
    owned_grad = partial + lax.ppermute(partial, "section", swap)
    first = beta_first * state[1] + (1.0 - beta_first) * owned_grad
    second = beta_second * state[2] + (1.0 - beta_second) * owned_grad * owned_grad
    both_steps = first / (jnp.sqrt(second) + epsilon)
    both_layers = (state[0] - learn_rate * both_steps).astype(jnp.bfloat16)
    adam_step = lax.dynamic_slice_in_dim(both_steps, layer, 1, axis=0)
    collected = lax.all_to_all(
        jnp.broadcast_to(both_layers[None], (owners, 2, piece_len)),
        "dp",
        split_axis=0,
        concat_axis=0,
        tiled=True,
    )
    new_weights = collected.transpose(1, 0, 2).reshape(2, owners * piece_len)
    return (adam_step, new_weights)


def solution(mesh):
    placed = (
        P("dp", None, None, None),
        P("dp", None),
        P("dp", None),
        P(("dp", "section")),
        P(("dp", "section")),
        P(("dp", "section"), None),
        P(),
        P(),
        P("section", "dp"),
        P("section", "dp"),
        P("section", "dp"),
    )
    return jax.shard_map(
        per_device, mesh=mesh, in_specs=placed, out_specs=(P("section", "dp"), P()), check_vma=False
    )
```

```python
import jax
import jax.numpy as jnp
from jax import lax
from jax.sharding import PartitionSpec as P

constant_entropy_scale = 0.5
trust_weight = 0.5
beta_first = 0.9
beta_second = 0.999
epsilon = 1e-08
learn_rate = 0.0001


def tap_stack(field):
    grid_side = field.shape[1]
    padded_rows = jnp.pad(field, ((0, 0), (1, 1), (1, 1), (0, 0)))
    return jnp.concatenate(
        [
            padded_rows[:, shift_row : shift_row + grid_side, shift_col : shift_col + grid_side, :]
            for shift_row in range(3)
            for shift_col in range(3)
        ],
        axis=-1,
    )


def conv_taps(field, kernel):
    channels = field.shape[3]
    return lax.conv_general_dilated(
        field,
        kernel.reshape(3, 3, channels, -1),
        (1, 1),
        ((1, 1), (1, 1)),
        dimension_numbers=("NHWC", "HWIO", "NHWC"),
        preferred_element_type=jnp.float32,
    )


def conv_kernel_grad(field, out_grad):
    numbers = lax.ConvDimensionNumbers(
        lhs_spec=(3, 0, 1, 2), rhs_spec=(3, 0, 1, 2), out_spec=(2, 3, 0, 1)
    )
    grad = lax.conv_general_dilated(
        field,
        out_grad,
        (1, 1),
        ((1, 1), (1, 1)),
        dimension_numbers=numbers,
        preferred_element_type=jnp.float32,
    )
    return grad.reshape(9 * field.shape[3], out_grad.shape[3])


def layer_grads(
    features,
    move_return_estimates,
    reference_policy_entries,
    actions,
    row_scale,
    w_first,
    second_weight,
    head,
):
    row_count, grid_side, _, channels = features.shape
    positions = row_count * grid_side * grid_side
    hidden = jax.nn.relu(conv_taps(features, w_first)).astype(jnp.bfloat16)
    summed = features.reshape(positions, channels).astype(jnp.float32) + conv_taps(
        hidden, second_weight
    ).reshape(positions, channels)
    block_out = jax.nn.relu(summed).astype(jnp.bfloat16)
    averaged_embedding = jnp.mean(
        block_out.astype(jnp.float32).reshape(row_count, grid_side * grid_side, channels), axis=1
    ).astype(jnp.bfloat16)
    logits = reference_policy_entries.astype(jnp.float32) + jnp.dot(
        averaged_embedding, head, preferred_element_type=jnp.float32
    )
    policy = jax.nn.softmax(logits, axis=-1)
    prior = jax.nn.softmax(reference_policy_entries.astype(jnp.float32), axis=-1)
    selected_moves = (actions[:, :, None] == jnp.arange(head.shape[1])[None, None, :]).astype(
        jnp.float32
    )
    move_logit_matrix = (
        jnp.einsum("vlu,vu->vl", selected_moves, move_return_estimates.astype(jnp.float32))
        / constant_entropy_scale
    )
    sample_weight = jax.nn.softmax(move_logit_matrix, axis=-1)
    logit_grad = (
        (1.0 + trust_weight) * policy
        - jnp.einsum("nk,nka->na", sample_weight, selected_moves)
        - trust_weight * prior
    ) * row_scale[:, None]
    pooled_grad = jnp.dot(logit_grad, head.astype(jnp.float32).T, precision=lax.Precision.HIGHEST)
    spread = jnp.broadcast_to(
        (pooled_grad / (grid_side * grid_side))[:, None, :],
        (row_count, grid_side * grid_side, channels),
    ).reshape(positions, channels)
    out_grad = jnp.where(block_out > 0, spread, 0.0).astype(jnp.bfloat16)
    grad_second = conv_kernel_grad(hidden, out_grad.reshape(features.shape))
    flipped = (
        second_weight.reshape(9, channels, channels)[::-1]
        .transpose(0, 2, 1)
        .reshape(9 * channels, channels)
    )
    hidden_grad = jnp.where(
        hidden > 0, conv_taps(out_grad.reshape(features.shape), flipped), 0.0
    ).astype(jnp.bfloat16)
    grad_first = conv_kernel_grad(features, hidden_grad)
    return (grad_first, grad_second)


def per_device(
    replay_rows,
    qvalues,
    target_logits,
    replay_owner,
    replay_slot,
    sample_actions,
    weights,
    head,
    master,
    moment_first,
    moment_second,
):
    rows_dev = replay_owner.shape[0]
    owners = lax.axis_size("dp")
    capacity = 2 * rows_dev // owners
    learn_rows = rows_dev * owners * lax.axis_size("section")
    channels = replay_rows.shape[3]
    w_first = weights[0].reshape(9 * channels, channels)
    second_weight = weights[1].reshape(9 * channels, channels)
    layer = lax.axis_index("section")
    swap = [(0, 1), (1, 0)]
    own_state = jnp.concatenate([master, moment_first, moment_second])
    partner_state = lax.ppermute(own_state, "section", swap)
    state = jnp.where(
        layer == 0,
        jnp.stack([own_state, partner_state], axis=1),
        jnp.stack([partner_state, own_state], axis=1),
    )
    row_order = jnp.arange(rows_dev, dtype=jnp.int32)
    earlier = (replay_owner[None, :] == replay_owner[:, None]) & (
        row_order[None, :] < row_order[:, None]
    )
    rank_within = jnp.sum(earlier.astype(jnp.int32), axis=1)
    slot_index = replay_owner * capacity + rank_within
    matches = slot_index[None, :] == jnp.arange(owners * capacity, dtype=jnp.int32)[:, None]
    occupied_entries = jnp.any(matches, axis=1)
    source = jnp.sum(jnp.where(matches, row_order[None, :], 0), axis=1)
    request = jnp.where(occupied_entries, jnp.take(replay_slot, source), -1).reshape(
        owners, capacity
    )
    row_index = jnp.maximum(
        lax.all_to_all(request, "dp", split_axis=0, concat_axis=0, tiled=True), 0
    )
    row_width = replay_rows.shape[1] * replay_rows.shape[2] * channels
    actions_n = qvalues.shape[1]
    side = jnp.concatenate(
        [
            jnp.take(qvalues, row_index, axis=0),
            jnp.take(target_logits, row_index, axis=0),
            jnp.zeros(row_index.shape + (channels - 2 * actions_n,), qvalues.dtype),
        ],
        axis=-1,
    )
    packed = jnp.concatenate(
        [jnp.take(replay_rows.reshape(-1, row_width), row_index, axis=0), side], axis=-1
    )
    slots = lax.all_to_all(packed, "dp", split_axis=0, concat_axis=0, tiled=True)
    picked = jnp.take(slots.reshape(owners * capacity, -1), slot_index, axis=0)
    features = picked[:, :row_width].reshape((rows_dev,) + replay_rows.shape[1:])
    move_return_estimates = picked[:, row_width : row_width + actions_n]
    reference_policy_entries = picked[:, row_width + actions_n : row_width + 2 * actions_n]
    row_scale = jnp.full((rows_dev,), 1.0 / learn_rows, jnp.float32)
    grad_first, grad_second = layer_grads(
        features,
        move_return_estimates,
        reference_policy_entries,
        sample_actions,
        row_scale,
        w_first,
        second_weight,
        head,
    )
    loss_derivative = jnp.stack([grad_first.reshape(-1), grad_second.reshape(-1)])
    piece_len = loss_derivative.shape[1] // owners
    contributions = lax.all_to_all(
        loss_derivative.reshape(2, owners, piece_len).transpose(1, 0, 2),
        "dp",
        split_axis=0,
        concat_axis=0,
        tiled=True,
    )
    partial = jnp.sum(contributions, axis=0)
    owned_grad = partial + lax.ppermute(partial, "section", swap)
    first = beta_first * state[1] + (1.0 - beta_first) * owned_grad
    second = beta_second * state[2] + (1.0 - beta_second) * owned_grad * owned_grad
    both_steps = first / (jnp.sqrt(second) + epsilon)
    both_layers = (state[0] - learn_rate * both_steps).astype(jnp.bfloat16)
    adam_step = lax.dynamic_slice_in_dim(both_steps, layer, 1, axis=0)
    collected = lax.all_to_all(
        jnp.broadcast_to(both_layers[None], (owners, 2, piece_len)),
        "dp",
        split_axis=0,
        concat_axis=0,
        tiled=True,
    )
    new_weights = collected.transpose(1, 0, 2).reshape(2, owners * piece_len)
    return (adam_step, new_weights)


def solution(mesh):
    placed = (
        P("dp", None, None, None),
        P("dp", None),
        P("dp", None),
        P(("dp", "section")),
        P(("dp", "section")),
        P(("dp", "section"), None),
        P(),
        P(),
        P("section", "dp"),
        P("section", "dp"),
        P("section", "dp"),
    )
    return jax.shard_map(
        per_device, mesh=mesh, in_specs=placed, out_specs=(P("section", "dp"), P()), check_vma=False
    )
```

```python
import jax
import jax.numpy as jnp
from jax import lax
from jax.sharding import PartitionSpec as P

constant_entropy_scale = 0.5
trust_weight = 0.5
beta_first = 0.9
beta_second = 0.999
epsilon = 1e-08
learn_rate = 0.0001


def tap_stack(field):
    grid_side = field.shape[1]
    padded_rows = jnp.pad(field, ((0, 0), (1, 1), (1, 1), (0, 0)))
    return jnp.concatenate(
        [
            padded_rows[:, shift_row : shift_row + grid_side, shift_col : shift_col + grid_side, :]
            for shift_row in range(3)
            for shift_col in range(3)
        ],
        axis=-1,
    )


def conv_taps(field, kernel):
    channels = field.shape[3]
    return lax.conv_general_dilated(
        field,
        kernel.reshape(3, 3, channels, -1),
        (1, 1),
        ((1, 1), (1, 1)),
        dimension_numbers=("NHWC", "HWIO", "NHWC"),
        preferred_element_type=jnp.float32,
    )


def conv_kernel_grad(field, out_grad):
    numbers = lax.ConvDimensionNumbers(
        lhs_spec=(3, 0, 1, 2), rhs_spec=(3, 0, 1, 2), out_spec=(2, 3, 0, 1)
    )
    grad = lax.conv_general_dilated(
        field,
        out_grad,
        (1, 1),
        ((1, 1), (1, 1)),
        dimension_numbers=numbers,
        preferred_element_type=jnp.float32,
    )
    return grad.reshape(9 * field.shape[3], out_grad.shape[3])


def layer_grads(
    features,
    move_return_estimates,
    reference_policy_entries,
    actions,
    row_scale,
    w_first,
    second_weight,
    head,
):
    row_count, grid_side, _, channels = features.shape
    positions = row_count * grid_side * grid_side
    hidden = jax.nn.relu(conv_taps(features, w_first)).astype(jnp.bfloat16)
    summed = features.reshape(positions, channels).astype(jnp.float32) + conv_taps(
        hidden, second_weight
    ).reshape(positions, channels)
    block_out = jax.nn.relu(summed).astype(jnp.bfloat16)
    averaged_embedding = jnp.mean(
        block_out.astype(jnp.float32).reshape(row_count, grid_side * grid_side, channels), axis=1
    ).astype(jnp.bfloat16)
    logits = reference_policy_entries.astype(jnp.float32) + jnp.dot(
        averaged_embedding, head, preferred_element_type=jnp.float32
    )
    policy = jax.nn.softmax(logits, axis=-1)
    prior = jax.nn.softmax(reference_policy_entries.astype(jnp.float32), axis=-1)
    selected_moves = (actions[:, :, None] == jnp.arange(head.shape[1])[None, None, :]).astype(
        jnp.float32
    )
    move_logit_matrix = (
        jnp.einsum("vlu,vu->vl", selected_moves, move_return_estimates.astype(jnp.float32))
        / constant_entropy_scale
    )
    sample_weight = jax.nn.softmax(move_logit_matrix, axis=-1)
    logit_grad = (
        (1.0 + trust_weight) * policy
        - jnp.einsum("nk,nka->na", sample_weight, selected_moves)
        - trust_weight * prior
    ) * row_scale[:, None]
    pooled_grad = jnp.dot(logit_grad, head.astype(jnp.float32).T, precision=lax.Precision.HIGHEST)
    spread = jnp.broadcast_to(
        (pooled_grad / (grid_side * grid_side))[:, None, :],
        (row_count, grid_side * grid_side, channels),
    ).reshape(positions, channels)
    out_grad = jnp.where(block_out > 0, spread, 0.0).astype(jnp.bfloat16)
    grad_second = conv_kernel_grad(hidden, out_grad.reshape(features.shape))
    flipped = (
        second_weight.reshape(9, channels, channels)[::-1]
        .transpose(0, 2, 1)
        .reshape(9 * channels, channels)
    )
    hidden_grad = jnp.where(
        hidden > 0, conv_taps(out_grad.reshape(features.shape), flipped), 0.0
    ).astype(jnp.bfloat16)
    grad_first = conv_kernel_grad(features, hidden_grad)
    return (grad_first, grad_second)


def per_device(
    replay_rows,
    qvalues,
    target_logits,
    replay_owner,
    replay_slot,
    sample_actions,
    weights,
    head,
    master,
    moment_first,
    moment_second,
):
    rows_dev = replay_owner.shape[0]
    owners = lax.axis_size("dp")
    capacity = 2 * rows_dev // owners
    learn_rows = rows_dev * owners * lax.axis_size("section")
    channels = replay_rows.shape[3]
    w_first = weights[0].reshape(9 * channels, channels)
    second_weight = weights[1].reshape(9 * channels, channels)
    layer = lax.axis_index("section")
    swap = [(0, 1), (1, 0)]
    own_state = jnp.concatenate([master, moment_first, moment_second])
    partner_state = lax.ppermute(own_state, "section", swap)
    state = jnp.where(
        layer == 0,
        jnp.stack([own_state, partner_state], axis=1),
        jnp.stack([partner_state, own_state], axis=1),
    )
    row_order = jnp.arange(rows_dev, dtype=jnp.int32)
    earlier = (replay_owner[None, :] == replay_owner[:, None]) & (
        row_order[None, :] < row_order[:, None]
    )
    rank_within = jnp.sum(earlier.astype(jnp.int32), axis=1)
    slot_index = replay_owner * capacity + rank_within
    matches = slot_index[None, :] == jnp.arange(owners * capacity, dtype=jnp.int32)[:, None]
    occupied_entries = jnp.any(matches, axis=1)
    source = jnp.sum(jnp.where(matches, row_order[None, :], 0), axis=1)
    request = jnp.where(occupied_entries, jnp.take(replay_slot, source), -1).reshape(
        owners, capacity
    )
    row_index = jnp.maximum(
        lax.all_to_all(request, "dp", split_axis=0, concat_axis=0, tiled=True), 0
    )
    grid_rows, grid_cols = replay_rows.shape[1], replay_rows.shape[2]
    actions_n = qvalues.shape[1]
    side = jnp.concatenate(
        [
            jnp.take(qvalues, row_index, axis=0),
            jnp.take(target_logits, row_index, axis=0),
            jnp.zeros(row_index.shape + (channels - 2 * actions_n,), qvalues.dtype),
        ],
        axis=-1,
    )
    side = jnp.pad(side[:, :, None, None, :], ((0, 0), (0, 0), (0, 0), (0, grid_cols - 1), (0, 0)))
    packed = jnp.concatenate([jnp.take(replay_rows, row_index, axis=0), side], axis=2)
    slots = lax.all_to_all(packed, "dp", split_axis=0, concat_axis=0, tiled=True)
    picked = jnp.take(
        slots.reshape((owners * capacity,) + slots.shape[2:]), slot_index, axis=0
    )
    features = picked[:, :grid_rows]
    move_return_estimates = picked[:, grid_rows, 0, :actions_n]
    reference_policy_entries = picked[:, grid_rows, 0, actions_n : 2 * actions_n]
    row_scale = jnp.full((rows_dev,), 1.0 / learn_rows, jnp.float32)
    grad_first, grad_second = layer_grads(
        features,
        move_return_estimates,
        reference_policy_entries,
        sample_actions,
        row_scale,
        w_first,
        second_weight,
        head,
    )
    loss_derivative = jnp.stack([grad_first.reshape(-1), grad_second.reshape(-1)])
    piece_len = loss_derivative.shape[1] // owners
    contributions = lax.all_to_all(
        loss_derivative.reshape(2, owners, piece_len).transpose(1, 0, 2),
        "dp",
        split_axis=0,
        concat_axis=0,
        tiled=True,
    )
    partial = jnp.sum(contributions, axis=0)
    owned_grad = partial + lax.ppermute(partial, "section", swap)
    first = beta_first * state[1] + (1.0 - beta_first) * owned_grad
    second = beta_second * state[2] + (1.0 - beta_second) * owned_grad * owned_grad
    both_steps = first / (jnp.sqrt(second) + epsilon)
    both_layers = (state[0] - learn_rate * both_steps).astype(jnp.bfloat16)
    adam_step = lax.dynamic_slice_in_dim(both_steps, layer, 1, axis=0)
    collected = lax.all_to_all(
        jnp.broadcast_to(both_layers[None], (owners, 2, piece_len)),
        "dp",
        split_axis=0,
        concat_axis=0,
        tiled=True,
    )
    new_weights = collected.transpose(1, 0, 2).reshape(2, owners * piece_len)
    return (adam_step, new_weights)


def solution(mesh):
    placed = (
        P("dp", None, None, None),
        P("dp", None),
        P("dp", None),
        P(("dp", "section")),
        P(("dp", "section")),
        P(("dp", "section"), None),
        P(),
        P(),
        P("section", "dp"),
        P("section", "dp"),
        P("section", "dp"),
    )
    return jax.shard_map(
        per_device, mesh=mesh, in_specs=placed, out_specs=(P("section", "dp"), P()), check_vma=False
    )
```

```python
import jax
import jax.numpy as jnp
from jax import lax
from jax.sharding import PartitionSpec as P

constant_entropy_scale = 0.5
trust_weight = 0.5
beta_first = 0.9
beta_second = 0.999
epsilon = 1e-08
learn_rate = 0.0001


def tap_stack(field):
    grid_side = field.shape[1]
    padded_rows = jnp.pad(field, ((0, 0), (1, 1), (1, 1), (0, 0)))
    return jnp.concatenate(
        [
            padded_rows[:, shift_row : shift_row + grid_side, shift_col : shift_col + grid_side, :]
            for shift_row in range(3)
            for shift_col in range(3)
        ],
        axis=-1,
    )


def conv_taps(field, kernel):
    channels = field.shape[3]
    return lax.conv_general_dilated(
        field,
        kernel.reshape(3, 3, channels, -1),
        (1, 1),
        ((1, 1), (1, 1)),
        dimension_numbers=("NHWC", "HWIO", "NHWC"),
        preferred_element_type=jnp.float32,
    )


def conv_kernel_grad(field, out_grad):
    numbers = lax.ConvDimensionNumbers(
        lhs_spec=(3, 0, 1, 2), rhs_spec=(3, 0, 1, 2), out_spec=(2, 3, 0, 1)
    )
    grad = lax.conv_general_dilated(
        field,
        out_grad,
        (1, 1),
        ((1, 1), (1, 1)),
        dimension_numbers=numbers,
        preferred_element_type=jnp.float32,
    )
    return grad.reshape(9 * field.shape[3], out_grad.shape[3])


def layer_grads(
    features,
    move_return_estimates,
    reference_policy_entries,
    actions,
    row_scale,
    w_first,
    second_weight,
    head,
):
    row_count, grid_side, _, channels = features.shape
    positions = row_count * grid_side * grid_side
    hidden = jax.nn.relu(conv_taps(features, w_first)).astype(jnp.bfloat16)
    summed = features.reshape(positions, channels).astype(jnp.float32) + conv_taps(
        hidden, second_weight
    ).reshape(positions, channels)
    block_out = jax.nn.relu(summed).astype(jnp.bfloat16)
    averaged_embedding = jnp.mean(
        block_out.astype(jnp.float32).reshape(row_count, grid_side * grid_side, channels), axis=1
    ).astype(jnp.bfloat16)
    logits = reference_policy_entries.astype(jnp.float32) + jnp.dot(
        averaged_embedding, head, preferred_element_type=jnp.float32
    )
    policy = jax.nn.softmax(logits, axis=-1)
    prior = jax.nn.softmax(reference_policy_entries.astype(jnp.float32), axis=-1)
    selected_moves = (actions[:, :, None] == jnp.arange(head.shape[1])[None, None, :]).astype(
        jnp.float32
    )
    move_logit_matrix = (
        jnp.einsum("vlu,vu->vl", selected_moves, move_return_estimates.astype(jnp.float32))
        / constant_entropy_scale
    )
    sample_weight = jax.nn.softmax(move_logit_matrix, axis=-1)
    logit_grad = (
        (1.0 + trust_weight) * policy
        - jnp.einsum("nk,nka->na", sample_weight, selected_moves)
        - trust_weight * prior
    ) * row_scale[:, None]
    pooled_grad = jnp.dot(logit_grad, head.astype(jnp.float32).T, precision=lax.Precision.HIGHEST)
    spread = jnp.broadcast_to(
        (pooled_grad / (grid_side * grid_side))[:, None, :],
        (row_count, grid_side * grid_side, channels),
    ).reshape(positions, channels)
    out_grad = jnp.where(block_out > 0, spread, 0.0).astype(jnp.bfloat16)
    grad_second = conv_kernel_grad(hidden, out_grad.reshape(features.shape))
    flipped = (
        second_weight.reshape(9, channels, channels)[::-1]
        .transpose(0, 2, 1)
        .reshape(9 * channels, channels)
    )
    hidden_grad = jnp.where(
        hidden > 0, conv_taps(out_grad.reshape(features.shape), flipped), 0.0
    ).astype(jnp.bfloat16)
    grad_first = conv_kernel_grad(features, hidden_grad)
    return (grad_first, grad_second)


def per_device(
    replay_rows,
    qvalues,
    target_logits,
    replay_owner,
    replay_slot,
    sample_actions,
    weights,
    head,
    master,
    moment_first,
    moment_second,
):
    rows_dev = replay_owner.shape[0]
    owners = lax.axis_size("dp")
    capacity = 2 * rows_dev // owners
    learn_rows = rows_dev * owners * lax.axis_size("section")
    channels = replay_rows.shape[3]
    w_first = weights[0].reshape(9 * channels, channels)
    second_weight = weights[1].reshape(9 * channels, channels)
    layer = lax.axis_index("section")
    swap = [(0, 1), (1, 0)]
    own_state = jnp.concatenate([master, moment_first, moment_second])
    partner_state = lax.ppermute(own_state, "section", swap)
    state = jnp.where(
        layer == 0,
        jnp.stack([own_state, partner_state], axis=1),
        jnp.stack([partner_state, own_state], axis=1),
    )
    row_order = jnp.arange(rows_dev, dtype=jnp.int32)
    earlier = (replay_owner[None, :] == replay_owner[:, None]) & (
        row_order[None, :] < row_order[:, None]
    )
    rank_within = jnp.sum(earlier.astype(jnp.int32), axis=1)
    slot_index = replay_owner * capacity + rank_within
    matches = slot_index[None, :] == jnp.arange(owners * capacity, dtype=jnp.int32)[:, None]
    occupied_entries = jnp.any(matches, axis=1)
    source = jnp.sum(jnp.where(matches, row_order[None, :], 0), axis=1)
    request = jnp.where(occupied_entries, jnp.take(replay_slot, source), -1).reshape(
        owners, capacity
    )
    row_index = jnp.maximum(
        lax.all_to_all(request, "dp", split_axis=0, concat_axis=0, tiled=True), 0
    )
    row_width = replay_rows.shape[1] * replay_rows.shape[2] * channels
    actions_n = qvalues.shape[1]
    table = jnp.concatenate(
        [
            replay_rows.reshape(-1, row_width),
            qvalues,
            target_logits,
            jnp.zeros((qvalues.shape[0], channels - 2 * actions_n), qvalues.dtype),
        ],
        axis=-1,
    )
    packed = jnp.take(table, row_index, axis=0)
    slots = lax.all_to_all(packed, "dp", split_axis=0, concat_axis=0, tiled=True)
    picked = jnp.take(slots.reshape(owners * capacity, -1), slot_index, axis=0)
    features = picked[:, :row_width].reshape((rows_dev,) + replay_rows.shape[1:])
    move_return_estimates = picked[:, row_width : row_width + actions_n]
    reference_policy_entries = picked[:, row_width + actions_n : row_width + 2 * actions_n]
    row_scale = jnp.full((rows_dev,), 1.0 / learn_rows, jnp.float32)
    grad_first, grad_second = layer_grads(
        features,
        move_return_estimates,
        reference_policy_entries,
        sample_actions,
        row_scale,
        w_first,
        second_weight,
        head,
    )
    loss_derivative = jnp.stack([grad_first.reshape(-1), grad_second.reshape(-1)])
    piece_len = loss_derivative.shape[1] // owners
    contributions = lax.all_to_all(
        loss_derivative.reshape(2, owners, piece_len).transpose(1, 0, 2),
        "dp",
        split_axis=0,
        concat_axis=0,
        tiled=True,
    )
    partial = jnp.sum(contributions, axis=0)
    owned_grad = partial + lax.ppermute(partial, "section", swap)
    first = beta_first * state[1] + (1.0 - beta_first) * owned_grad
    second = beta_second * state[2] + (1.0 - beta_second) * owned_grad * owned_grad
    both_steps = first / (jnp.sqrt(second) + epsilon)
    both_layers = (state[0] - learn_rate * both_steps).astype(jnp.bfloat16)
    adam_step = lax.dynamic_slice_in_dim(both_steps, layer, 1, axis=0)
    collected = lax.all_to_all(
        jnp.broadcast_to(both_layers[None], (owners, 2, piece_len)),
        "dp",
        split_axis=0,
        concat_axis=0,
        tiled=True,
    )
    new_weights = collected.transpose(1, 0, 2).reshape(2, owners * piece_len)
    return (adam_step, new_weights)


def solution(mesh):
    placed = (
        P("dp", None, None, None),
        P("dp", None),
        P("dp", None),
        P(("dp", "section")),
        P(("dp", "section")),
        P(("dp", "section"), None),
        P(),
        P(),
        P("section", "dp"),
        P("section", "dp"),
        P("section", "dp"),
    )
    return jax.shard_map(
        per_device, mesh=mesh, in_specs=placed, out_specs=(P("section", "dp"), P()), check_vma=False
    )
```

```python
import jax
import jax.numpy as jnp
from jax import lax
from jax.sharding import PartitionSpec as P

constant_entropy_scale = 0.5
trust_weight = 0.5
beta_first = 0.9
beta_second = 0.999
epsilon = 1e-08
learn_rate = 0.0001


def tap_stack(field):
    grid_side = field.shape[1]
    padded_rows = jnp.pad(field, ((0, 0), (1, 1), (1, 1), (0, 0)))
    return jnp.concatenate(
        [
            padded_rows[:, shift_row : shift_row + grid_side, shift_col : shift_col + grid_side, :]
            for shift_row in range(3)
            for shift_col in range(3)
        ],
        axis=-1,
    )


def conv_taps(field, kernel):
    channels = field.shape[3]
    return lax.conv_general_dilated(
        field,
        kernel.reshape(3, 3, channels, -1),
        (1, 1),
        ((1, 1), (1, 1)),
        dimension_numbers=("NHWC", "HWIO", "NHWC"),
        preferred_element_type=jnp.float32,
    )


def conv_kernel_grad(field, out_grad):
    numbers = lax.ConvDimensionNumbers(
        lhs_spec=(3, 0, 1, 2), rhs_spec=(3, 0, 1, 2), out_spec=(2, 3, 0, 1)
    )
    grad = lax.conv_general_dilated(
        field,
        out_grad,
        (1, 1),
        ((1, 1), (1, 1)),
        dimension_numbers=numbers,
        preferred_element_type=jnp.float32,
    )
    return grad.reshape(9 * field.shape[3], out_grad.shape[3])


def layer_grads(
    features,
    move_return_estimates,
    reference_policy_entries,
    actions,
    row_scale,
    w_first,
    second_weight,
    head,
):
    row_count, grid_side, _, channels = features.shape
    positions = row_count * grid_side * grid_side
    hidden = jax.nn.relu(conv_taps(features, w_first)).astype(jnp.bfloat16)
    summed = features.reshape(positions, channels).astype(jnp.float32) + conv_taps(
        hidden, second_weight
    ).reshape(positions, channels)
    block_out = jax.nn.relu(summed).astype(jnp.bfloat16)
    averaged_embedding = jnp.mean(
        block_out.astype(jnp.float32).reshape(row_count, grid_side * grid_side, channels), axis=1
    ).astype(jnp.bfloat16)
    logits = reference_policy_entries.astype(jnp.float32) + jnp.dot(
        averaged_embedding, head, preferred_element_type=jnp.float32
    )
    policy = jax.nn.softmax(logits, axis=-1)
    prior = jax.nn.softmax(reference_policy_entries.astype(jnp.float32), axis=-1)
    selected_moves = (actions[:, :, None] == jnp.arange(head.shape[1])[None, None, :]).astype(
        jnp.float32
    )
    move_logit_matrix = (
        jnp.einsum("vlu,vu->vl", selected_moves, move_return_estimates.astype(jnp.float32))
        / constant_entropy_scale
    )
    sample_weight = jax.nn.softmax(move_logit_matrix, axis=-1)
    logit_grad = (
        (1.0 + trust_weight) * policy
        - jnp.einsum("nk,nka->na", sample_weight, selected_moves)
        - trust_weight * prior
    ) * row_scale[:, None]
    pooled_grad = jnp.dot(logit_grad, head.astype(jnp.float32).T, precision=lax.Precision.HIGHEST)
    spread = jnp.broadcast_to(
        (pooled_grad / (grid_side * grid_side))[:, None, :],
        (row_count, grid_side * grid_side, channels),
    ).reshape(positions, channels)
    out_grad = jnp.where(block_out > 0, spread, 0.0).astype(jnp.bfloat16)
    grad_second = conv_kernel_grad(hidden, out_grad.reshape(features.shape))
    flipped = (
        second_weight.reshape(9, channels, channels)[::-1]
        .transpose(0, 2, 1)
        .reshape(9 * channels, channels)
    )
    hidden_grad = jnp.where(
        hidden > 0, conv_taps(out_grad.reshape(features.shape), flipped), 0.0
    ).astype(jnp.bfloat16)
    grad_first = conv_kernel_grad(features, hidden_grad)
    return (grad_first, grad_second)


def per_device(
    replay_rows,
    qvalues,
    target_logits,
    replay_owner,
    replay_slot,
    sample_actions,
    weights,
    head,
    master,
    moment_first,
    moment_second,
):
    rows_dev = replay_owner.shape[0]
    owners = lax.axis_size("dp")
    capacity = 2 * rows_dev // owners
    learn_rows = rows_dev * owners * lax.axis_size("section")
    channels = replay_rows.shape[3]
    w_first = weights[0].reshape(9 * channels, channels)
    second_weight = weights[1].reshape(9 * channels, channels)
    layer = lax.axis_index("section")
    swap = [(0, 1), (1, 0)]
    own_state = jnp.concatenate([master, moment_first, moment_second])
    partner_state = lax.ppermute(own_state, "section", swap)
    state = jnp.where(
        layer == 0,
        jnp.stack([own_state, partner_state], axis=1),
        jnp.stack([partner_state, own_state], axis=1),
    )
    row_order = jnp.arange(rows_dev, dtype=jnp.int32)
    earlier = (replay_owner[None, :] == replay_owner[:, None]) & (
        row_order[None, :] < row_order[:, None]
    )
    rank_within = jnp.sum(earlier.astype(jnp.int32), axis=1)
    slot_index = replay_owner * capacity + rank_within
    matches = slot_index[None, :] == jnp.arange(owners * capacity, dtype=jnp.int32)[:, None]
    request = jnp.sum(jnp.where(matches, replay_slot[None, :], 0), axis=1).reshape(
        owners, capacity
    )
    row_index = jnp.maximum(
        lax.all_to_all(request, "dp", split_axis=0, concat_axis=0, tiled=True), 0
    )
    row_width = replay_rows.shape[1] * replay_rows.shape[2] * channels
    actions_n = qvalues.shape[1]
    table = jnp.concatenate(
        [
            replay_rows.reshape(-1, row_width),
            qvalues,
            target_logits,
            jnp.zeros((qvalues.shape[0], channels - 2 * actions_n), qvalues.dtype),
        ],
        axis=-1,
    )
    packed = jnp.take(table, row_index, axis=0)
    slots = lax.all_to_all(packed, "dp", split_axis=0, concat_axis=0, tiled=True)
    picked = jnp.take(slots.reshape(owners * capacity, -1), slot_index, axis=0)
    features = picked[:, :row_width].reshape((rows_dev,) + replay_rows.shape[1:])
    move_return_estimates = picked[:, row_width : row_width + actions_n]
    reference_policy_entries = picked[:, row_width + actions_n : row_width + 2 * actions_n]
    row_scale = jnp.full((rows_dev,), 1.0 / learn_rows, jnp.float32)
    grad_first, grad_second = layer_grads(
        features,
        move_return_estimates,
        reference_policy_entries,
        sample_actions,
        row_scale,
        w_first,
        second_weight,
        head,
    )
    loss_derivative = jnp.stack([grad_first.reshape(-1), grad_second.reshape(-1)])
    piece_len = loss_derivative.shape[1] // owners
    contributions = lax.all_to_all(
        loss_derivative.reshape(2, owners, piece_len).transpose(1, 0, 2),
        "dp",
        split_axis=0,
        concat_axis=0,
        tiled=True,
    )
    partial = jnp.sum(contributions, axis=0)
    owned_grad = partial + lax.ppermute(partial, "section", swap)
    first = beta_first * state[1] + (1.0 - beta_first) * owned_grad
    second = beta_second * state[2] + (1.0 - beta_second) * owned_grad * owned_grad
    both_steps = first / (jnp.sqrt(second) + epsilon)
    both_layers = (state[0] - learn_rate * both_steps).astype(jnp.bfloat16)
    adam_step = lax.dynamic_slice_in_dim(both_steps, layer, 1, axis=0)
    collected = lax.all_to_all(
        jnp.broadcast_to(both_layers[None], (owners, 2, piece_len)),
        "dp",
        split_axis=0,
        concat_axis=0,
        tiled=True,
    )
    new_weights = collected.transpose(1, 0, 2).reshape(2, owners * piece_len)
    return (adam_step, new_weights)


def solution(mesh):
    placed = (
        P("dp", None, None, None),
        P("dp", None),
        P("dp", None),
        P(("dp", "section")),
        P(("dp", "section")),
        P(("dp", "section"), None),
        P(),
        P(),
        P("section", "dp"),
        P("section", "dp"),
        P("section", "dp"),
    )
    return jax.shard_map(
        per_device, mesh=mesh, in_specs=placed, out_specs=(P("section", "dp"), P()), check_vma=False
    )
```

```python
import jax
import jax.numpy as jnp
from jax import lax
from jax.sharding import PartitionSpec as P

constant_entropy_scale = 0.5
trust_weight = 0.5
beta_first = 0.9
beta_second = 0.999
epsilon = 1e-08
learn_rate = 0.0001


def tap_stack(field):
    grid_side = field.shape[1]
    padded_rows = jnp.pad(field, ((0, 0), (1, 1), (1, 1), (0, 0)))
    return jnp.concatenate(
        [
            padded_rows[:, shift_row : shift_row + grid_side, shift_col : shift_col + grid_side, :]
            for shift_row in range(3)
            for shift_col in range(3)
        ],
        axis=-1,
    )


def conv_taps(field, kernel):
    channels = field.shape[3]
    return lax.conv_general_dilated(
        field,
        kernel.reshape(3, 3, channels, -1),
        (1, 1),
        ((1, 1), (1, 1)),
        dimension_numbers=("NHWC", "HWIO", "NHWC"),
        preferred_element_type=jnp.float32,
    )


def conv_kernel_grad(field, out_grad):
    numbers = lax.ConvDimensionNumbers(
        lhs_spec=(3, 0, 1, 2), rhs_spec=(3, 0, 1, 2), out_spec=(2, 3, 0, 1)
    )
    grad = lax.conv_general_dilated(
        field,
        out_grad,
        (1, 1),
        ((1, 1), (1, 1)),
        dimension_numbers=numbers,
        preferred_element_type=jnp.float32,
    )
    return grad.reshape(9 * field.shape[3], out_grad.shape[3])


def layer_grads(
    features,
    move_return_estimates,
    reference_policy_entries,
    actions,
    row_scale,
    w_first,
    second_weight,
    head,
):
    row_count, grid_side, _, channels = features.shape
    positions = row_count * grid_side * grid_side
    hidden = jax.nn.relu(conv_taps(features, w_first)).astype(jnp.bfloat16)
    summed = features.reshape(positions, channels).astype(jnp.float32) + conv_taps(
        hidden, second_weight
    ).reshape(positions, channels)
    block_out = jax.nn.relu(summed).astype(jnp.bfloat16)
    averaged_embedding = jnp.mean(
        block_out.astype(jnp.float32).reshape(row_count, grid_side * grid_side, channels), axis=1
    ).astype(jnp.bfloat16)
    logits = reference_policy_entries.astype(jnp.float32) + jnp.dot(
        averaged_embedding, head, preferred_element_type=jnp.float32
    )
    policy = jax.nn.softmax(logits, axis=-1)
    prior = jax.nn.softmax(reference_policy_entries.astype(jnp.float32), axis=-1)
    selected_moves = (actions[:, :, None] == jnp.arange(head.shape[1])[None, None, :]).astype(
        jnp.float32
    )
    move_logit_matrix = (
        jnp.einsum("vlu,vu->vl", selected_moves, move_return_estimates.astype(jnp.float32))
        / constant_entropy_scale
    )
    sample_weight = jax.nn.softmax(move_logit_matrix, axis=-1)
    logit_grad = (
        (1.0 + trust_weight) * policy
        - jnp.einsum("nk,nka->na", sample_weight, selected_moves)
        - trust_weight * prior
    ) * row_scale[:, None]
    pooled_grad = jnp.dot(logit_grad, head.astype(jnp.float32).T, precision=lax.Precision.HIGHEST)
    spread = jnp.broadcast_to(
        (pooled_grad / (grid_side * grid_side))[:, None, :],
        (row_count, grid_side * grid_side, channels),
    ).reshape(positions, channels)
    out_grad = jnp.where(block_out > 0, spread, 0.0).astype(jnp.bfloat16)
    grad_second = conv_kernel_grad(hidden, out_grad.reshape(features.shape))
    flipped = (
        second_weight.reshape(9, channels, channels)[::-1]
        .transpose(0, 2, 1)
        .reshape(9 * channels, channels)
    )
    hidden_grad = jnp.where(
        hidden > 0, conv_taps(out_grad.reshape(features.shape), flipped), 0.0
    ).astype(jnp.bfloat16)
    grad_first = conv_kernel_grad(features, hidden_grad)
    return (grad_first, grad_second)


def per_device(
    replay_rows,
    qvalues,
    target_logits,
    replay_owner,
    replay_slot,
    sample_actions,
    weights,
    head,
    master,
    moment_first,
    moment_second,
):
    rows_dev = replay_owner.shape[0]
    owners = lax.axis_size("dp")
    capacity = 2 * rows_dev // owners
    learn_rows = rows_dev * owners * lax.axis_size("section")
    channels = replay_rows.shape[3]
    w_first = weights[0].reshape(9 * channels, channels)
    second_weight = weights[1].reshape(9 * channels, channels)
    layer = lax.axis_index("section")
    swap = [(0, 1), (1, 0)]
    own_state = jnp.concatenate([master, moment_first, moment_second])
    partner_state = lax.ppermute(own_state, "section", swap)
    state = jnp.where(
        layer == 0,
        jnp.stack([own_state, partner_state], axis=1),
        jnp.stack([partner_state, own_state], axis=1),
    )
    row_order = jnp.arange(rows_dev, dtype=jnp.int32)
    earlier = (replay_owner[None, :] == replay_owner[:, None]) & (
        row_order[None, :] < row_order[:, None]
    )
    rank_within = jnp.sum(earlier.astype(jnp.int32), axis=1)
    slot_index = replay_owner * capacity + rank_within
    matches = slot_index[None, :] == jnp.arange(owners * capacity, dtype=jnp.int32)[:, None]
    request = jnp.sum(jnp.where(matches, replay_slot[None, :], 0), axis=1).reshape(
        owners, capacity
    )
    row_width = replay_rows.shape[1] * replay_rows.shape[2] * channels
    actions_n = qvalues.shape[1]
    table = jnp.concatenate(
        [
            replay_rows.reshape(-1, row_width),
            qvalues,
            target_logits,
            jnp.zeros((qvalues.shape[0], channels - 2 * actions_n), qvalues.dtype),
        ],
        axis=-1,
    )
    table, request = lax.optimization_barrier((table, request))
    row_index = jnp.maximum(
        lax.all_to_all(request, "dp", split_axis=0, concat_axis=0, tiled=True), 0
    )
    packed = jnp.take(table, row_index, axis=0)
    slots = lax.all_to_all(packed, "dp", split_axis=0, concat_axis=0, tiled=True)
    picked = jnp.take(slots.reshape(owners * capacity, -1), slot_index, axis=0)
    features = picked[:, :row_width].reshape((rows_dev,) + replay_rows.shape[1:])
    move_return_estimates = picked[:, row_width : row_width + actions_n]
    reference_policy_entries = picked[:, row_width + actions_n : row_width + 2 * actions_n]
    row_scale = jnp.full((rows_dev,), 1.0 / learn_rows, jnp.float32)
    grad_first, grad_second = layer_grads(
        features,
        move_return_estimates,
        reference_policy_entries,
        sample_actions,
        row_scale,
        w_first,
        second_weight,
        head,
    )
    loss_derivative = jnp.stack([grad_first.reshape(-1), grad_second.reshape(-1)])
    piece_len = loss_derivative.shape[1] // owners
    contributions = lax.all_to_all(
        loss_derivative.reshape(2, owners, piece_len).transpose(1, 0, 2),
        "dp",
        split_axis=0,
        concat_axis=0,
        tiled=True,
    )
    partial = jnp.sum(contributions, axis=0)
    owned_grad = partial + lax.ppermute(partial, "section", swap)
    first = beta_first * state[1] + (1.0 - beta_first) * owned_grad
    second = beta_second * state[2] + (1.0 - beta_second) * owned_grad * owned_grad
    both_steps = first / (jnp.sqrt(second) + epsilon)
    both_layers = (state[0] - learn_rate * both_steps).astype(jnp.bfloat16)
    adam_step = lax.dynamic_slice_in_dim(both_steps, layer, 1, axis=0)
    collected = lax.all_to_all(
        jnp.broadcast_to(both_layers[None], (owners, 2, piece_len)),
        "dp",
        split_axis=0,
        concat_axis=0,
        tiled=True,
    )
    new_weights = collected.transpose(1, 0, 2).reshape(2, owners * piece_len)
    return (adam_step, new_weights)


def solution(mesh):
    placed = (
        P("dp", None, None, None),
        P("dp", None),
        P("dp", None),
        P(("dp", "section")),
        P(("dp", "section")),
        P(("dp", "section"), None),
        P(),
        P(),
        P("section", "dp"),
        P("section", "dp"),
        P("section", "dp"),
    )
    return jax.shard_map(
        per_device, mesh=mesh, in_specs=placed, out_specs=(P("section", "dp"), P()), check_vma=False
    )
```

```python
import jax
import jax.numpy as jnp
from jax import lax
from jax.sharding import PartitionSpec as P

constant_entropy_scale = 0.5
trust_weight = 0.5
beta_first = 0.9
beta_second = 0.999
epsilon = 1e-08
learn_rate = 0.0001


def tap_stack(field):
    grid_side = field.shape[1]
    padded_rows = jnp.pad(field, ((0, 0), (1, 1), (1, 1), (0, 0)))
    return jnp.concatenate(
        [
            padded_rows[:, shift_row : shift_row + grid_side, shift_col : shift_col + grid_side, :]
            for shift_row in range(3)
            for shift_col in range(3)
        ],
        axis=-1,
    )


def conv_taps(field, kernel):
    channels = field.shape[3]
    return lax.conv_general_dilated(
        field,
        kernel.reshape(3, 3, channels, -1),
        (1, 1),
        ((1, 1), (1, 1)),
        dimension_numbers=("NHWC", "HWIO", "NHWC"),
        preferred_element_type=jnp.float32,
    )


def conv_kernel_grad(field, out_grad):
    numbers = lax.ConvDimensionNumbers(
        lhs_spec=(3, 0, 1, 2), rhs_spec=(3, 0, 1, 2), out_spec=(2, 3, 0, 1)
    )
    grad = lax.conv_general_dilated(
        field,
        out_grad,
        (1, 1),
        ((1, 1), (1, 1)),
        dimension_numbers=numbers,
        preferred_element_type=jnp.float32,
    )
    return grad.reshape(9 * field.shape[3], out_grad.shape[3])


def layer_grads(
    features,
    move_return_estimates,
    reference_policy_entries,
    actions,
    row_scale,
    w_first,
    second_weight,
    head,
):
    row_count, grid_side, _, channels = features.shape
    positions = row_count * grid_side * grid_side
    hidden = jax.nn.relu(conv_taps(features, w_first)).astype(jnp.bfloat16)
    summed = features.reshape(positions, channels).astype(jnp.float32) + conv_taps(
        hidden, second_weight
    ).reshape(positions, channels)
    block_out = jax.nn.relu(summed).astype(jnp.bfloat16)
    averaged_embedding = jnp.mean(
        block_out.astype(jnp.float32).reshape(row_count, grid_side * grid_side, channels), axis=1
    ).astype(jnp.bfloat16)
    logits = reference_policy_entries.astype(jnp.float32) + jnp.dot(
        averaged_embedding, head, preferred_element_type=jnp.float32
    )
    policy = jax.nn.softmax(logits, axis=-1)
    prior = jax.nn.softmax(reference_policy_entries.astype(jnp.float32), axis=-1)
    selected_moves = (actions[:, :, None] == jnp.arange(head.shape[1])[None, None, :]).astype(
        jnp.float32
    )
    move_logit_matrix = (
        jnp.einsum("vlu,vu->vl", selected_moves, move_return_estimates.astype(jnp.float32))
        / constant_entropy_scale
    )
    sample_weight = jax.nn.softmax(move_logit_matrix, axis=-1)
    logit_grad = (
        (1.0 + trust_weight) * policy
        - jnp.einsum("nk,nka->na", sample_weight, selected_moves)
        - trust_weight * prior
    ) * row_scale[:, None]
    pooled_grad = jnp.dot(logit_grad, head.astype(jnp.float32).T, precision=lax.Precision.HIGHEST)
    spread = jnp.broadcast_to(
        (pooled_grad / (grid_side * grid_side))[:, None, :],
        (row_count, grid_side * grid_side, channels),
    ).reshape(positions, channels)
    out_grad = jnp.where(block_out > 0, spread, 0.0).astype(jnp.bfloat16)
    grad_second = conv_kernel_grad(hidden, out_grad.reshape(features.shape))
    flipped = (
        second_weight.reshape(9, channels, channels)[::-1]
        .transpose(0, 2, 1)
        .reshape(9 * channels, channels)
    )
    hidden_grad = jnp.where(
        hidden > 0, conv_taps(out_grad.reshape(features.shape), flipped), 0.0
    ).astype(jnp.bfloat16)
    grad_first = conv_kernel_grad(features, hidden_grad)
    return (grad_first, grad_second)


def per_device(
    replay_rows,
    qvalues,
    target_logits,
    replay_owner,
    replay_slot,
    sample_actions,
    weights,
    head,
    master,
    moment_first,
    moment_second,
):
    rows_dev = replay_owner.shape[0]
    owners = lax.axis_size("dp")
    capacity = 2 * rows_dev // owners
    learn_rows = rows_dev * owners * lax.axis_size("section")
    channels = replay_rows.shape[3]
    w_first = weights[0].reshape(9 * channels, channels)
    second_weight = weights[1].reshape(9 * channels, channels)
    layer = lax.axis_index("section")
    swap = [(0, 1), (1, 0)]
    own_state = jnp.concatenate([master, moment_first, moment_second])
    partner_state = lax.ppermute(own_state, "section", swap)
    state = jnp.where(
        layer == 0,
        jnp.stack([own_state, partner_state], axis=1),
        jnp.stack([partner_state, own_state], axis=1),
    )
    row_order = jnp.arange(rows_dev, dtype=jnp.int32)
    earlier = (replay_owner[None, :] == replay_owner[:, None]) & (
        row_order[None, :] < row_order[:, None]
    )
    rank_within = jnp.sum(earlier.astype(jnp.int32), axis=1)
    slot_index = replay_owner * capacity + rank_within
    matches = slot_index[None, :] == jnp.arange(owners * capacity, dtype=jnp.int32)[:, None]
    request = jnp.sum(jnp.where(matches, replay_slot[None, :], 0), axis=1).reshape(
        owners, capacity
    )
    row_index = lax.all_to_all(request, "dp", split_axis=0, concat_axis=0, tiled=True)
    row_width = replay_rows.shape[1] * replay_rows.shape[2] * channels
    actions_n = qvalues.shape[1]
    table = jnp.concatenate(
        [
            replay_rows.reshape(-1, row_width),
            qvalues,
            target_logits,
            jnp.zeros((qvalues.shape[0], channels - 2 * actions_n), qvalues.dtype),
        ],
        axis=-1,
    )
    packed = jnp.take(table, row_index, axis=0)
    slots = lax.all_to_all(packed, "dp", split_axis=0, concat_axis=0, tiled=True)
    picked = jnp.take(slots.reshape(owners * capacity, -1), slot_index, axis=0)
    features = picked[:, :row_width].reshape((rows_dev,) + replay_rows.shape[1:])
    move_return_estimates = picked[:, row_width : row_width + actions_n]
    reference_policy_entries = picked[:, row_width + actions_n : row_width + 2 * actions_n]
    row_scale = jnp.full((rows_dev,), 1.0 / learn_rows, jnp.float32)
    grad_first, grad_second = layer_grads(
        features,
        move_return_estimates,
        reference_policy_entries,
        sample_actions,
        row_scale,
        w_first,
        second_weight,
        head,
    )
    loss_derivative = jnp.stack([grad_first.reshape(-1), grad_second.reshape(-1)])
    piece_len = loss_derivative.shape[1] // owners
    contributions = lax.all_to_all(
        loss_derivative.reshape(2, owners, piece_len).transpose(1, 0, 2),
        "dp",
        split_axis=0,
        concat_axis=0,
        tiled=True,
    )
    partial = jnp.sum(contributions, axis=0)
    owned_grad = partial + lax.ppermute(partial, "section", swap)
    first = beta_first * state[1] + (1.0 - beta_first) * owned_grad
    second = beta_second * state[2] + (1.0 - beta_second) * owned_grad * owned_grad
    both_steps = first / (jnp.sqrt(second) + epsilon)
    both_layers = (state[0] - learn_rate * both_steps).astype(jnp.bfloat16)
    adam_step = lax.dynamic_slice_in_dim(both_steps, layer, 1, axis=0)
    collected = lax.all_to_all(
        jnp.broadcast_to(both_layers[None], (owners, 2, piece_len)),
        "dp",
        split_axis=0,
        concat_axis=0,
        tiled=True,
    )
    new_weights = collected.transpose(1, 0, 2).reshape(2, owners * piece_len)
    return (adam_step, new_weights)


def solution(mesh):
    placed = (
        P("dp", None, None, None),
        P("dp", None),
        P("dp", None),
        P(("dp", "section")),
        P(("dp", "section")),
        P(("dp", "section"), None),
        P(),
        P(),
        P("section", "dp"),
        P("section", "dp"),
        P("section", "dp"),
    )
    return jax.shard_map(
        per_device, mesh=mesh, in_specs=placed, out_specs=(P("section", "dp"), P()), check_vma=False
    )
```

```python
import jax
import jax.numpy as jnp
from jax import lax
from jax.sharding import PartitionSpec as P

constant_entropy_scale = 0.5
trust_weight = 0.5
beta_first = 0.9
beta_second = 0.999
epsilon = 1e-08
learn_rate = 0.0001


def tap_stack(field):
    grid_side = field.shape[1]
    padded_rows = jnp.pad(field, ((0, 0), (1, 1), (1, 1), (0, 0)))
    return jnp.concatenate(
        [
            padded_rows[:, shift_row : shift_row + grid_side, shift_col : shift_col + grid_side, :]
            for shift_row in range(3)
            for shift_col in range(3)
        ],
        axis=-1,
    )


def conv_taps(field, kernel):
    channels = field.shape[3]
    return lax.conv_general_dilated(
        field,
        kernel.reshape(3, 3, channels, -1),
        (1, 1),
        ((1, 1), (1, 1)),
        dimension_numbers=("NHWC", "HWIO", "NHWC"),
        preferred_element_type=jnp.float32,
    )


def conv_kernel_grad(field, out_grad):
    numbers = lax.ConvDimensionNumbers(
        lhs_spec=(3, 0, 1, 2), rhs_spec=(3, 0, 1, 2), out_spec=(2, 3, 0, 1)
    )
    grad = lax.conv_general_dilated(
        field,
        out_grad,
        (1, 1),
        ((1, 1), (1, 1)),
        dimension_numbers=numbers,
        preferred_element_type=jnp.float32,
    )
    return grad.reshape(9 * field.shape[3], out_grad.shape[3])


def layer_grads(
    features,
    move_return_estimates,
    reference_policy_entries,
    actions,
    row_scale,
    w_first,
    second_weight,
    head,
):
    row_count, grid_side, _, channels = features.shape
    positions = row_count * grid_side * grid_side
    hidden = jax.nn.relu(conv_taps(features, w_first)).astype(jnp.bfloat16)
    summed = features.reshape(positions, channels).astype(jnp.float32) + conv_taps(
        hidden, second_weight
    ).reshape(positions, channels)
    block_out = jax.nn.relu(summed).astype(jnp.bfloat16)
    averaged_embedding = jnp.mean(
        block_out.astype(jnp.float32).reshape(row_count, grid_side * grid_side, channels), axis=1
    ).astype(jnp.bfloat16)
    logits = reference_policy_entries.astype(jnp.float32) + jnp.dot(
        averaged_embedding, head, preferred_element_type=jnp.float32
    )
    policy = jax.nn.softmax(logits, axis=-1)
    prior = jax.nn.softmax(reference_policy_entries.astype(jnp.float32), axis=-1)
    selected_moves = (actions[:, :, None] == jnp.arange(head.shape[1])[None, None, :]).astype(
        jnp.float32
    )
    move_logit_matrix = (
        jnp.einsum("vlu,vu->vl", selected_moves, move_return_estimates.astype(jnp.float32))
        / constant_entropy_scale
    )
    sample_weight = jax.nn.softmax(move_logit_matrix, axis=-1)
    logit_grad = (
        (1.0 + trust_weight) * policy
        - jnp.einsum("nk,nka->na", sample_weight, selected_moves)
        - trust_weight * prior
    ) * row_scale[:, None]
    pooled_grad = jnp.dot(logit_grad, head.astype(jnp.float32).T, precision=lax.Precision.HIGHEST)
    spread = jnp.broadcast_to(
        (pooled_grad / (grid_side * grid_side))[:, None, :],
        (row_count, grid_side * grid_side, channels),
    ).reshape(positions, channels)
    out_grad = jnp.where(block_out > 0, spread, 0.0).astype(jnp.bfloat16)
    grad_second = conv_kernel_grad(hidden, out_grad.reshape(features.shape))
    flipped = (
        second_weight.reshape(9, channels, channels)[::-1]
        .transpose(0, 2, 1)
        .reshape(9 * channels, channels)
    )
    hidden_grad = jnp.where(
        hidden > 0, conv_taps(out_grad.reshape(features.shape), flipped), 0.0
    ).astype(jnp.bfloat16)
    grad_first = conv_kernel_grad(features, hidden_grad)
    return (grad_first, grad_second)


def per_device(
    replay_rows,
    qvalues,
    target_logits,
    replay_owner,
    replay_slot,
    sample_actions,
    weights,
    head,
    master,
    moment_first,
    moment_second,
):
    rows_dev = replay_owner.shape[0]
    owners = lax.axis_size("dp")
    capacity = 2 * rows_dev // owners
    learn_rows = rows_dev * owners * lax.axis_size("section")
    channels = replay_rows.shape[3]
    w_first = weights[0].reshape(9 * channels, channels)
    second_weight = weights[1].reshape(9 * channels, channels)
    layer = lax.axis_index("section")
    swap = [(0, 1), (1, 0)]
    own_state = jnp.concatenate([master, moment_first, moment_second])
    partner_state = lax.ppermute(own_state, "section", swap)
    state = jnp.where(
        layer == 0,
        jnp.stack([own_state, partner_state], axis=1),
        jnp.stack([partner_state, own_state], axis=1),
    )
    row_order = jnp.arange(rows_dev, dtype=jnp.int32)
    earlier = (replay_owner[None, :] == replay_owner[:, None]) & (
        row_order[None, :] < row_order[:, None]
    )
    rank_within = jnp.sum(earlier.astype(jnp.int32), axis=1)
    slot_index = replay_owner * capacity + rank_within
    matches = slot_index[None, :] == jnp.arange(owners * capacity, dtype=jnp.int32)[:, None]
    request = jnp.sum(jnp.where(matches, replay_slot[None, :], 0), axis=1).reshape(
        owners, capacity
    )
    row_index = lax.all_to_all(request, "dp", split_axis=0, concat_axis=0, tiled=True)
    row_width = replay_rows.shape[1] * replay_rows.shape[2] * channels
    actions_n = qvalues.shape[1]
    table = jnp.concatenate(
        [
            replay_rows.reshape(-1, row_width),
            qvalues,
            target_logits,
            jnp.zeros((qvalues.shape[0], channels - 2 * actions_n), qvalues.dtype),
        ],
        axis=-1,
    )
    packed = jnp.take(table, row_index, axis=0)
    slots = lax.all_to_all(packed, "dp", split_axis=0, concat_axis=0, tiled=True)
    picked = jnp.take(slots.reshape(owners * capacity, -1), slot_index, axis=0)
    features = picked[:, :row_width].reshape((rows_dev,) + replay_rows.shape[1:])
    move_return_estimates = picked[:, row_width : row_width + actions_n]
    reference_policy_entries = picked[:, row_width + actions_n : row_width + 2 * actions_n]
    row_scale = jnp.full((rows_dev,), 1.0 / learn_rows, jnp.float32)
    grad_first, grad_second = layer_grads(
        features,
        move_return_estimates,
        reference_policy_entries,
        sample_actions,
        row_scale,
        w_first,
        second_weight,
        head,
    )
    piece_len = grad_first.size // owners
    contributions = lax.all_to_all(
        jnp.concatenate(
            [grad_first.reshape(owners, piece_len), grad_second.reshape(owners, piece_len)],
            axis=1,
        ),
        "dp",
        split_axis=0,
        concat_axis=0,
        tiled=True,
    )
    partial = jnp.sum(contributions, axis=0).reshape(2, piece_len)
    owned_grad = partial + lax.ppermute(partial, "section", swap)
    first = beta_first * state[1] + (1.0 - beta_first) * owned_grad
    second = beta_second * state[2] + (1.0 - beta_second) * owned_grad * owned_grad
    both_steps = first / (jnp.sqrt(second) + epsilon)
    both_layers = (state[0] - learn_rate * both_steps).astype(jnp.bfloat16)
    adam_step = lax.dynamic_slice_in_dim(both_steps, layer, 1, axis=0)
    collected = lax.all_to_all(
        jnp.broadcast_to(both_layers[None], (owners, 2, piece_len)),
        "dp",
        split_axis=0,
        concat_axis=0,
        tiled=True,
    )
    new_weights = collected.transpose(1, 0, 2).reshape(2, owners * piece_len)
    return (adam_step, new_weights)


def solution(mesh):
    placed = (
        P("dp", None, None, None),
        P("dp", None),
        P("dp", None),
        P(("dp", "section")),
        P(("dp", "section")),
        P(("dp", "section"), None),
        P(),
        P(),
        P("section", "dp"),
        P("section", "dp"),
        P("section", "dp"),
    )
    return jax.shard_map(
        per_device, mesh=mesh, in_specs=placed, out_specs=(P("section", "dp"), P()), check_vma=False
    )
```

```python
import jax
import jax.numpy as jnp
from jax import lax
from jax.sharding import PartitionSpec as P

constant_entropy_scale = 0.5
trust_weight = 0.5
beta_first = 0.9
beta_second = 0.999
epsilon = 1e-08
learn_rate = 0.0001


def tap_stack(field):
    grid_side = field.shape[1]
    padded_rows = jnp.pad(field, ((0, 0), (1, 1), (1, 1), (0, 0)))
    return jnp.concatenate(
        [
            padded_rows[:, shift_row : shift_row + grid_side, shift_col : shift_col + grid_side, :]
            for shift_row in range(3)
            for shift_col in range(3)
        ],
        axis=-1,
    )


def conv_taps(field, kernel):
    channels = field.shape[3]
    return lax.conv_general_dilated(
        field,
        kernel.reshape(3, 3, channels, -1),
        (1, 1),
        ((1, 1), (1, 1)),
        dimension_numbers=("NHWC", "HWIO", "NHWC"),
        preferred_element_type=jnp.float32,
    )


def conv_kernel_grad(field, out_grad):
    numbers = lax.ConvDimensionNumbers(
        lhs_spec=(3, 0, 1, 2), rhs_spec=(3, 0, 1, 2), out_spec=(2, 3, 0, 1)
    )
    grad = lax.conv_general_dilated(
        field,
        out_grad,
        (1, 1),
        ((1, 1), (1, 1)),
        dimension_numbers=numbers,
        preferred_element_type=jnp.float32,
    )
    return grad.reshape(9 * field.shape[3], out_grad.shape[3])


def layer_grads(
    features,
    move_return_estimates,
    reference_policy_entries,
    actions,
    row_scale,
    w_first,
    second_weight,
    head,
):
    row_count, grid_side, _, channels = features.shape
    positions = row_count * grid_side * grid_side
    hidden = jax.nn.relu(conv_taps(features, w_first)).astype(jnp.bfloat16)
    summed = features.reshape(positions, channels).astype(jnp.float32) + conv_taps(
        hidden, second_weight
    ).reshape(positions, channels)
    block_out = jax.nn.relu(summed).astype(jnp.bfloat16)
    averaged_embedding = jnp.mean(
        block_out.astype(jnp.float32).reshape(row_count, grid_side * grid_side, channels), axis=1
    ).astype(jnp.bfloat16)
    logits = reference_policy_entries.astype(jnp.float32) + jnp.dot(
        averaged_embedding, head, preferred_element_type=jnp.float32
    )
    policy = jax.nn.softmax(logits, axis=-1)
    prior = jax.nn.softmax(reference_policy_entries.astype(jnp.float32), axis=-1)
    selected_moves = (actions[:, :, None] == jnp.arange(head.shape[1])[None, None, :]).astype(
        jnp.float32
    )
    move_logit_matrix = (
        jnp.einsum("vlu,vu->vl", selected_moves, move_return_estimates.astype(jnp.float32))
        / constant_entropy_scale
    )
    sample_weight = jax.nn.softmax(move_logit_matrix, axis=-1)
    logit_grad = (
        (1.0 + trust_weight) * policy
        - jnp.einsum("nk,nka->na", sample_weight, selected_moves)
        - trust_weight * prior
    ) * row_scale[:, None]
    pooled_grad = jnp.dot(logit_grad, head.astype(jnp.float32).T, precision=lax.Precision.HIGHEST)
    spread = jnp.broadcast_to(
        (pooled_grad / (grid_side * grid_side))[:, None, :],
        (row_count, grid_side * grid_side, channels),
    ).reshape(positions, channels)
    out_grad = jnp.where(block_out > 0, spread, 0.0).astype(jnp.bfloat16)
    grad_second = conv_kernel_grad(hidden, out_grad.reshape(features.shape))
    flipped = (
        second_weight.reshape(9, channels, channels)[::-1]
        .transpose(0, 2, 1)
        .reshape(9 * channels, channels)
    )
    hidden_grad = jnp.where(
        hidden > 0, conv_taps(out_grad.reshape(features.shape), flipped), 0.0
    ).astype(jnp.bfloat16)
    grad_first = conv_kernel_grad(features, hidden_grad)
    return (grad_first, grad_second)


def per_device(
    replay_rows,
    qvalues,
    target_logits,
    replay_owner,
    replay_slot,
    sample_actions,
    weights,
    head,
    master,
    moment_first,
    moment_second,
):
    rows_dev = replay_owner.shape[0]
    owners = lax.axis_size("dp")
    capacity = 2 * rows_dev // owners
    learn_rows = rows_dev * owners * lax.axis_size("section")
    channels = replay_rows.shape[3]
    w_first = weights[0].reshape(9 * channels, channels)
    second_weight = weights[1].reshape(9 * channels, channels)
    layer = lax.axis_index("section")
    swap = [(0, 1), (1, 0)]
    own_state = jnp.concatenate([master, moment_first, moment_second])
    partner_state = lax.ppermute(own_state, "section", swap)
    state = jnp.where(
        layer == 0,
        jnp.stack([own_state, partner_state], axis=1),
        jnp.stack([partner_state, own_state], axis=1),
    )
    row_order = jnp.arange(rows_dev, dtype=jnp.int32)
    earlier = (replay_owner[None, :] == replay_owner[:, None]) & (
        row_order[None, :] < row_order[:, None]
    )
    rank_within = jnp.sum(earlier.astype(jnp.int32), axis=1)
    slot_index = replay_owner * capacity + rank_within
    matches = slot_index[None, :] == jnp.arange(owners * capacity, dtype=jnp.int32)[:, None]
    request = jnp.sum(jnp.where(matches, replay_slot[None, :], 0), axis=1).reshape(
        owners, capacity
    )
    row_index = lax.all_to_all(request, "dp", split_axis=0, concat_axis=0, tiled=True)
    row_width = replay_rows.shape[1] * replay_rows.shape[2] * channels
    actions_n = qvalues.shape[1]
    table = jnp.concatenate(
        [
            replay_rows.reshape(-1, row_width),
            qvalues,
            target_logits,
        ],
        axis=-1,
    )
    packed = jnp.take(table, row_index, axis=0)
    slots = lax.all_to_all(packed, "dp", split_axis=0, concat_axis=0, tiled=True)
    picked = jnp.take(slots.reshape(owners * capacity, -1), slot_index, axis=0)
    features = picked[:, :row_width].reshape((rows_dev,) + replay_rows.shape[1:])
    move_return_estimates = picked[:, row_width : row_width + actions_n]
    reference_policy_entries = picked[:, row_width + actions_n : row_width + 2 * actions_n]
    row_scale = jnp.full((rows_dev,), 1.0 / learn_rows, jnp.float32)
    grad_first, grad_second = layer_grads(
        features,
        move_return_estimates,
        reference_policy_entries,
        sample_actions,
        row_scale,
        w_first,
        second_weight,
        head,
    )
    loss_derivative = jnp.stack([grad_first.reshape(-1), grad_second.reshape(-1)])
    piece_len = loss_derivative.shape[1] // owners
    contributions = lax.all_to_all(
        loss_derivative.reshape(2, owners, piece_len).transpose(1, 0, 2),
        "dp",
        split_axis=0,
        concat_axis=0,
        tiled=True,
    )
    partial = jnp.sum(contributions, axis=0)
    owned_grad = partial + lax.ppermute(partial, "section", swap)
    first = beta_first * state[1] + (1.0 - beta_first) * owned_grad
    second = beta_second * state[2] + (1.0 - beta_second) * owned_grad * owned_grad
    both_steps = first / (jnp.sqrt(second) + epsilon)
    both_layers = (state[0] - learn_rate * both_steps).astype(jnp.bfloat16)
    adam_step = lax.dynamic_slice_in_dim(both_steps, layer, 1, axis=0)
    collected = lax.all_to_all(
        jnp.broadcast_to(both_layers[None], (owners, 2, piece_len)),
        "dp",
        split_axis=0,
        concat_axis=0,
        tiled=True,
    )
    new_weights = collected.transpose(1, 0, 2).reshape(2, owners * piece_len)
    return (adam_step, new_weights)


def solution(mesh):
    placed = (
        P("dp", None, None, None),
        P("dp", None),
        P("dp", None),
        P(("dp", "section")),
        P(("dp", "section")),
        P(("dp", "section"), None),
        P(),
        P(),
        P("section", "dp"),
        P("section", "dp"),
        P("section", "dp"),
    )
    return jax.shard_map(
        per_device, mesh=mesh, in_specs=placed, out_specs=(P("section", "dp"), P()), check_vma=False
    )
```
